128 devices in a mesh: req: 16 (over z, y), exp: 8 (over x, core).
Axes of the slice: x: 4, y: 4, z: 4, core: 2. Of those that a mesh axis runs over, the one named last changes fastest.
Arguments:
- residual: bfloat16 [16384, 2048], P(('req', 'exp')), may hold values from -3 to 3
- query_vectors: bfloat16 [16384, 2048], P(('req', 'exp')), may hold values from -12 to 12
- key_vectors: bfloat16 [16384, 2048], P(('req', 'exp')), may hold values from -12 to 12
- value_vectors: bfloat16 [16384, 2048], P(('req', 'exp')), may hold values from -6 to 6
- segment_ids: int32 [16384], P('req'), may hold values from 0 to 2, as said below
- prompt_lengths: int32 [16, 3], replicated, may hold values from 1 to 512, as said below
- request_groups: int32 [16], replicated, may hold values from 0 to 15, as said below
- page_table: int32 [16, 8], replicated, may hold values from 0 to 127, as said below
- expert_ids: int32 [16384, 8], P(('req', 'exp')), may hold values from 0 to 63, all different within a row; in each aligned block of 128 rows (0 to 127, 128 to 255, ...) at most 24 rows name the same one
- gate_weights: float32 [16384, 8], P(('req', 'exp')), may hold values from 0.1 to 0.6
- out_weight: bfloat16 [2048, 2048], replicated, may hold values from -0.125 to 0.125
- norm_gain: float32 [2048], replicated, may hold values from 0.5 to 2
- expert_inner: bfloat16 [128, 2048, 1024], P(('req', 'exp')), may hold values from -0.125 to 0.125
- expert_outer: bfloat16 [128, 512, 2048], P(('req', 'exp')), may hold values from -0.1875 to 0.1875
Outputs:
- layer_out: bfloat16 [16384, 2048], P(('req', 'exp'))
- kv_pages: bfloat16 [128, 2, 128, 2048], P('req', None, None, 'exp')
The draws below stay inside these ranges and needn't reach their ends.
Inputs may be any that keep to these rules, and one draw needn't show every extreme that they name: `prompt_lengths`: each row sums to 1024, and its largest entry is 512. `segment_ids`: within each group of 1024 rows the numbers never fall; prompt j of the request r with request_groups[r] = g fills prompt_lengths[r, j] consecutive rows of group g. `request_groups`: each group appears once. `page_table`: all entries differ; the 8 pages of one request lie in 8 different owner groups, the owner of slot s being s // 8. `expert_ids`: the 8 ids of a token differ; among the 128 tokens of one device no expert is named more than 24 times, a bound that some block reaches.
All inputs are finite; a program needn't handle non-finite values.
Results may differ from the reference program's by a relative error of at most 0.013.
Values may be sent and summed in bfloat16 or wider, within the bound.
No kernel may reach another device: no remote copies, remote signals or barrier semaphores. Data moves between devices by JAX's collectives and lax.ppermute only.
A program may use at most 192 MiB of HBM per device.

```python
import math
import jax
import jax.numpy as jnp
import numpy as np
from jax import lax

D = 2048
HEADS = 16
HEAD = 128
FF = 1024
TOP = 8
TOK_DEV = 128
PAGE = 128
SEGS = 3
HD = 2048
EXPERTS = 64
TOK_GRP = 1024
TOKENS = 16384
PAGES_REQ = 8
SLOTS = 128
PROMPT_MAX = 512
CAP = 24
N_REQ = 16
DEVICES = 128


def request_layout(key):
    key_perm = jax.random.fold_in(key, 7001)
    key_longest = jax.random.fold_in(key, 7002)
    key_weight = jax.random.fold_in(key, 7003)
    key_offset = jax.random.fold_in(key, 7004)
    key_local = jax.random.fold_in(key, 7005)
    groups_of = jax.random.permutation(key_perm, N_REQ).astype(jnp.int32)
    longest = jax.random.randint(key_longest, (N_REQ,), 0, SEGS)
    weights = jax.random.randint(key_weight, (N_REQ, SEGS), 1, 101)
    column = jnp.arange(SEGS)[None, :]
    is_longest = column == longest[:, None]
    weights = jnp.where(is_longest, 0, weights)
    spare_tokens = TOK_GRP - PROMPT_MAX - (SEGS - 1)
    shares = spare_tokens * weights // jnp.sum(weights, axis=1, keepdims=True)
    leftover = spare_tokens - jnp.sum(shares, axis=1, keepdims=True)
    extra_tokens = jnp.where(column == (longest[:, None] + 1) % SEGS, leftover, 0)
    group_lengths = jnp.where(is_longest, PROMPT_MAX, 1 + shares + extra_tokens).astype(jnp.int32)
    prompt_lengths = group_lengths[groups_of]
    prompt_ends = jnp.cumsum(group_lengths, axis=1)
    positions = jnp.arange(TOK_GRP)
    segment_ids = jnp.sum((positions[None, :, None] >= prompt_ends[:, None, :SEGS - 1]).astype(jnp.int32), axis=2).reshape(TOKENS)
    offsets = jax.random.permutation(key_offset, N_REQ)[:PAGES_REQ]
    owners = (jnp.arange(N_REQ)[:, None] + offsets[None, :]) % N_REQ
    local_keys = jax.random.split(key_local, N_REQ)
    local_order = jax.vmap(lambda one_key: jax.random.permutation(one_key, PAGES_REQ))(local_keys)
    local_slot = local_order[owners, jnp.arange(PAGES_REQ)[None, :]]
    page_table = (owners * PAGES_REQ + local_slot).astype(jnp.int32)
    return (groups_of, prompt_lengths.astype(jnp.int32), segment_ids.astype(jnp.int32), page_table)


def draw_request_groups(key, part):
    return request_layout(key)[0]


def draw_prompt_lengths(key, part):
    return request_layout(key)[1]


def draw_segment_ids(key, part):
    return request_layout(key)[2]


def draw_page_table(key, part):
    return request_layout(key)[3]


def query_key_pair(key):
    key_query = jax.random.fold_in(key, 8101)
    key_key = jax.random.fold_in(key, 8102)
    queries = 1.3 * jax.random.normal(key_query, (TOKENS, HD))
    keys = 1.3 * jax.random.normal(key_key, (TOKENS, HD))
    return (jnp.clip(queries, -12.0, 12.0).astype(jnp.float32), jnp.clip(keys, -12.0, 12.0).astype(jnp.float32))


def draw_query_vectors(key, part):
    return query_key_pair(key)[0].astype(jnp.bfloat16)


def draw_key_vectors(key, part):
    return query_key_pair(key)[1].astype(jnp.bfloat16)


def steps_of(stream_key, dims, cuts, least, high):
    def one(axis_at, shards_of):
        draws = jax.random.uniform(jax.random.fold_in(jax.random.fold_in(stream_key, 6), axis_at), (shards_of,), jnp.float32, least / len(cuts), high / len(cuts))
        return jnp.repeat(jnp.exp(draws), dims[axis_at] // shards_of).reshape((-1,) + (1,) * (len(dims) - axis_at - 1))

    level = one(*cuts[0])
    for cut in cuts[1:]:
        level = level * one(*cut)
    return level


def assign_block(stream_key, own, number, rows, count, top, limit, slope):
    sequence = jax.random.permutation(stream_key, count)
    heavy_load, ordinary = portions_of(count, rows * top, limit, slope, True), portions_of(count, rows * top, limit, slope, False)
    places = jnp.arange(count)

    def named(sizes, rotation):
        used = int((sizes > 0).sum())
        fixed = max(1, used // 4)
        shifted = fixed + (places - fixed + rotation * (used - fixed)) % max(1, count - fixed)
        return jnp.zeros((count,), jnp.int32).at[sequence[jnp.where(places < fixed, places, shifted)]].set(jnp.asarray(sizes, jnp.int32))

    sizes = jnp.where(number % 4 == 0, named(heavy_load, number // 4), named(ordinary, number - number // 4 - 1))
    mixed = jax.random.permutation(jax.random.fold_in(own, 3), count)
    donor, receiver = mixed[0:count // 2 * 2:2], mixed[1:count // 2 * 2:2]
    room = jnp.minimum(sizes[donor] - 1, limit - sizes[receiver]) // 2
    room = jnp.where((donor == sequence[0]) | (receiver == sequence[0]) | (sizes[receiver] == 0), 0, jnp.maximum(room, 0))
    shifted = jax.random.randint(jax.random.fold_in(own, 4), (count // 2,), 0, 1 << 20) % (room + 1)
    sizes = sizes.at[donor].add(-shifted).at[receiver].add(shifted)
    labels = jnp.searchsorted(jnp.cumsum(sizes), jnp.arange(rows * top), side="right").astype(jnp.int32)
    grid = labels.reshape(top, rows).T
    grid = grid[jax.random.permutation(jax.random.fold_in(own, 1), rows)]
    rotation = jax.random.randint(jax.random.fold_in(own, 2), (rows, 1), 0, top)
    return jnp.take_along_axis(grid, (jnp.arange(top)[None, :] + rotation) % top, axis=1)


def portions_of(count, total, reach, slope, full):
    weights = [(1 << 20) // math.isqrt(grade ** slope) + 1 for grade in range(1, count + 1)]
    largest = reach if full else min(reach, max(-(-total // count), total * weights[0] // sum(weights)))
    least = 1 if total - largest >= count - 1 else 0
    given, surplus = [largest] + [least] * (count - 1), total - largest - least * (count - 1)
    while surplus > 0:
        movable = [i for i in range(1, count) if given[i] < largest] or [i for i in range(1, count) if given[i] < reach]
        whole, budget = sum([weights[i] for i in movable]), surplus
        for i in movable:
            addition = min(reach - given[i], max(1, budget * weights[i] // whole), surplus)
            given[i] = given[i] + addition
            surplus = surplus - addition
    return np.array(given)


def noise(rng, shape, width, limit, shards=(), held_as=jnp.bfloat16):
    values = width * jax.random.normal(rng, shape, jnp.float32)
    if shards:
        values = values * steps_of(rng, shape, shards, -0.22, 0.18)
    return jnp.clip(values, -limit, limit).astype(held_as)


def setup_inputs(seed: int = 0) -> dict:
    arg_keys = jax.random.split(jax.random.key(seed), 15)
    residual = noise(arg_keys[0], (TOKENS, D), 0.5, 3.0, ((0, 128),))
    query_vectors = draw_query_vectors(jax.random.fold_in(arg_keys[14], 71), 0)
    key_vectors = draw_key_vectors(jax.random.fold_in(arg_keys[14], 71), 0)
    value_vectors = noise(arg_keys[3], (TOKENS, HD), 1.0, 6.0, ((0, 128),))
    segment_ids = draw_segment_ids(jax.random.fold_in(arg_keys[14], 71), 0)
    prompt_lengths = draw_prompt_lengths(jax.random.fold_in(arg_keys[14], 71), 0)
    request_groups = draw_request_groups(jax.random.fold_in(arg_keys[14], 71), 0)
    page_table = draw_page_table(jax.random.fold_in(arg_keys[14], 71), 0)
    expert_ids_keys = jax.random.split(jax.random.fold_in(arg_keys[8], 1), TOKENS // TOK_DEV)
    expert_ids_turns = jax.random.permutation(jax.random.fold_in(arg_keys[8], 3), TOKENS // TOK_DEV)
    expert_ids = jax.vmap(lambda own, number: assign_block(jax.random.fold_in(arg_keys[8], 2), own, number, TOK_DEV, EXPERTS, TOP, CAP, 2))(expert_ids_keys, expert_ids_turns).reshape((TOKENS, TOP))
    gate_weights = jnp.clip(jnp.exp(math.log(0.6) - 1.7917595 * jax.random.uniform(arg_keys[9], (TOKENS, TOP), jnp.float32) ** steps_of(arg_keys[9], (TOKENS, TOP), ((0, 128),), -0.2, 0.2)), 0.1, 0.6)
    out_weight = noise(arg_keys[10], (HD, D), HD ** -0.5, 0.125)
    norm_gain = jnp.clip(jnp.exp(jax.random.uniform(arg_keys[11], (D,), jnp.float32, math.log(0.5), math.log(2.0))), 0.5, 2.0)
    expert_inner = noise(arg_keys[12], (2 * EXPERTS, D, FF), D ** -0.5, 0.125, ((0, 128),))
    expert_outer = noise(arg_keys[13], (2 * EXPERTS, FF // 2, D), FF ** -0.5, 0.1875, ((0, 128),))
    return dict(residual=residual, query_vectors=query_vectors, key_vectors=key_vectors, value_vectors=value_vectors, segment_ids=segment_ids, prompt_lengths=prompt_lengths, request_groups=request_groups, page_table=page_table, expert_ids=expert_ids, gate_weights=gate_weights, out_weight=out_weight, norm_gain=norm_gain, expert_inner=expert_inner, expert_outer=expert_outer)


rope_base = 10000.0
norm_eps = 1e-06
masked_score = -1e+30

def rotate(values_in, positions):
    row_count = values_in.shape[0]
    half_head = HEAD // 2
    inverse = rope_base ** (-(2.0 * jnp.arange(half_head, dtype=jnp.float32)) / HEAD)
    angles = positions[:, None] * inverse[None, :]
    cosine = jnp.cos(angles)[:, None, :]
    sines = jnp.sin(angles)[:, None, :]
    shaped = values_in.astype(jnp.float32).reshape(row_count, -1, HEAD)
    first_half = shaped[..., :half_head]
    second_half = shaped[..., half_head:]
    turned = jnp.concatenate([first_half * cosine - second_half * sines, second_half * cosine + first_half * sines], axis=-1)
    return turned.reshape(row_count, -1).astype(jnp.bfloat16)

def group_attention(operands):
    query_rows, key_rows, value_rows, group_segments = operands
    scores = jnp.einsum('qhd,khd->hqk', query_rows.astype(jnp.float32), key_rows.astype(jnp.float32)) * HEAD ** (-0.5)
    same_prompt = (group_segments[:, None] == group_segments[None, :])[None]
    scores = jnp.where(same_prompt, scores, masked_score)
    top_score = lax.optimization_barrier(jnp.max(scores, axis=-1, keepdims=True))
    weights = jnp.where(same_prompt, jnp.exp(scores - top_score), 0.0)
    totals = lax.optimization_barrier(jnp.sum(weights, axis=-1))
    rounded = lax.optimization_barrier(weights.astype(jnp.bfloat16))
    mixed = jnp.einsum('hqk,khd->qhd', rounded.astype(jnp.float32), value_rows.astype(jnp.float32))
    return (mixed / totals.T[:, :, None]).astype(jnp.bfloat16).reshape(TOK_GRP, HD)

def reference(residual, query_vectors, key_vectors, value_vectors, segment_ids, prompt_lengths, request_groups, page_table, expert_ids, gate_weights, out_weight, norm_gain, expert_inner, expert_outer):
    groups = jnp.arange(N_REQ, dtype=jnp.int32)
    holds_request = (request_groups[None, :] == groups[:, None]).astype(jnp.int32)
    group_lengths = lax.optimization_barrier(jnp.sum(holds_request[:, :, None] * prompt_lengths[None, :, :], axis=1))
    group_pages = lax.optimization_barrier(jnp.sum(holds_request[:, :, None] * page_table[None, :, :], axis=1))
    starts = jnp.cumsum(group_lengths, axis=1) - group_lengths
    segments = segment_ids.reshape(N_REQ, TOK_GRP)
    prompt_index = jnp.arange(prompt_lengths.shape[1], dtype=jnp.int32)
    token_start = lax.optimization_barrier(jnp.sum(jnp.where(segments[:, :, None] == prompt_index[None, None, :], starts[:, None, :], 0), axis=2))
    positions = (jnp.arange(TOK_GRP, dtype=jnp.int32)[None, :] - token_start).reshape(TOKENS).astype(jnp.float32)
    query_turned = rotate(query_vectors, positions)
    key_turned = rotate(key_vectors, positions)
    stacked = jnp.stack([key_turned.reshape(N_REQ * PAGES_REQ, PAGE, HD), value_vectors.reshape(N_REQ * PAGES_REQ, PAGE, HD)], axis=1)
    kv_pages = jnp.zeros((SLOTS, 2, PAGE, HD), jnp.bfloat16).at[group_pages.reshape(-1)].set(stacked)
    attention = lax.map(group_attention, (query_turned.reshape(N_REQ, TOK_GRP, HEADS, HEAD), key_turned.reshape(N_REQ, TOK_GRP, HEADS, HEAD), value_vectors.reshape(N_REQ, TOK_GRP, HEADS, HEAD), segments)).reshape(TOKENS, HD)
    hidden = residual.astype(jnp.float32) + jnp.dot(attention, out_weight, preferred_element_type=jnp.float32)
    normed = (hidden * lax.rsqrt(lax.optimization_barrier(jnp.mean(hidden * hidden, axis=-1, keepdims=True)) + norm_eps) * norm_gain).astype(jnp.bfloat16)
    expert_range = jnp.arange(EXPERTS, dtype=jnp.int32)
    chosen = (expert_ids[:, :, None] == expert_range[None, None, :]).astype(jnp.int32)
    picked = lax.optimization_barrier(jnp.sum(chosen, axis=1))
    earlier = jnp.cumsum(picked, axis=0) - picked
    expert_rank = lax.optimization_barrier(jnp.sum(chosen * earlier[:, None, :], axis=2))
    capacity_rows = DEVICES * CAP
    token_index = jnp.broadcast_to(jnp.arange(TOKENS, dtype=jnp.int32)[:, None], expert_ids.shape)
    slot_table = jnp.full((EXPERTS, capacity_rows), TOKENS, jnp.int32).at[expert_ids, expert_rank].set(token_index)
    padded = jnp.concatenate([normed, jnp.zeros((1, D), jnp.bfloat16)], axis=0)

    def expert_step(accumulated, operands):
        expert, inner_pair, outer_pair, slot_tokens = operands
        gathered = padded[slot_tokens]
        partial_sums = []
        for half_index in range(2):
            projected = jnp.dot(gathered, inner_pair[half_index], preferred_element_type=jnp.float32)
            half_units = projected.shape[1] // 2
            active = (jax.nn.silu(projected[:, :half_units]) * projected[:, half_units:]).astype(jnp.bfloat16)
            partial_sums.append(jnp.dot(active, outer_pair[half_index], preferred_element_type=jnp.float32))
        expert_out = (partial_sums[0] + partial_sums[1]).astype(jnp.bfloat16)
        weight_row = lax.optimization_barrier(jnp.sum(jnp.where(expert_ids == expert, gate_weights, 0.0), axis=1))
        weight_pad = jnp.concatenate([weight_row, jnp.zeros((1,), jnp.float32)])
        accumulated = accumulated.at[slot_tokens].add(weight_pad[slot_tokens][:, None] * expert_out.astype(jnp.float32))
        return (accumulated, None)
    accumulated, unused = lax.scan(expert_step, jnp.zeros((TOKENS + 1, D), jnp.float32), (expert_range, expert_inner.reshape(EXPERTS, 2, D, FF), expert_outer.reshape(EXPERTS, 2, FF // 2, D), slot_table))
    layer_out = (hidden + accumulated[:TOKENS]).astype(jnp.bfloat16)
    return (layer_out, kv_pages)
```

```python
import jax
import jax.numpy as jnp
from jax import lax
from jax.sharding import PartitionSpec as P

HEAD = 128
PAGE = 128


rope_base = 10000.0
norm_eps = 1e-06
masked_score = -1e30


def partner(value, axis, distance):
    return lax.ppermute(value, axis, [(i, i ^ 1 << distance) for i in range(lax.axis_size(axis))])


def rotate(values_in, positions):
    row_count = values_in.shape[0]
    half_head = HEAD // 2
    inverse = rope_base ** (-(2.0 * jnp.arange(half_head, dtype=jnp.float32)) / HEAD)
    angles = positions[:, None] * inverse[None, :]
    cosine = jnp.cos(angles)[:, None, :]
    sines = jnp.sin(angles)[:, None, :]
    shaped = values_in.astype(jnp.float32).reshape(row_count, -1, HEAD)
    first_half = shaped[..., :half_head]
    second_half = shaped[..., half_head:]
    turned = jnp.concatenate(
        [first_half * cosine - second_half * sines, second_half * cosine + first_half * sines],
        axis=-1,
    )
    return turned.reshape(row_count, -1).astype(jnp.bfloat16)


def score_block(query_block, query_segments, key_block, key_segments):
    scores = jnp.einsum(
        "qhd,khd->hqk", query_block, key_block, preferred_element_type=jnp.float32
    ) * HEAD ** (-0.5)
    same_prompt = (query_segments[:, None] == key_segments[None, :])[None]
    return (jnp.where(same_prompt, scores, masked_score), same_prompt)


def attend_all(query_heads, key_heads, value_heads, group_segments, block_rows):
    block_count = query_heads.shape[0] // block_rows

    def one_block(block_index):
        start_row = block_index * block_rows
        query_block = lax.dynamic_slice_in_dim(query_heads, start_row, block_rows, 0)
        query_segments = lax.dynamic_slice_in_dim(group_segments, start_row, block_rows, 0)
        scores, same_prompt = score_block(query_block, query_segments, key_heads, group_segments)
        top_score = jnp.max(scores, axis=-1, keepdims=True)
        weights = jnp.where(same_prompt, jnp.exp(scores - top_score), 0.0)
        totals = jnp.sum(weights, axis=-1)
        mixed = jnp.einsum(
            "hqk,khd->qhd",
            weights.astype(jnp.bfloat16),
            value_heads,
            preferred_element_type=jnp.float32,
        )
        return (mixed / totals.T[:, :, None]).astype(jnp.bfloat16)

    results = lax.map(one_block, jnp.arange(block_count))
    return results.reshape(query_heads.shape[0], -1)


def send_rows(blocks):
    arrived = lax.all_to_all(blocks, ("req", "exp"), split_axis=0, concat_axis=0, tiled=True)
    return arrived


def send_back(blocks):
    arrived = lax.all_to_all(blocks, ("req", "exp"), split_axis=0, concat_axis=0, tiled=True)
    return arrived


def to_chunks(blocks):
    count, rows, width = blocks.shape
    return blocks.reshape(count, 8, rows * width // 8)


def from_chunks(blocks, rows, width):
    return blocks.reshape(blocks.shape[0], rows, width)


def gated_units(rows, inner_half):
    projected = jnp.dot(rows, inner_half, preferred_element_type=jnp.float32)
    half_units = projected.shape[1] // 2
    return (jax.nn.silu(projected[:, :half_units]) * projected[:, half_units:]).astype(jnp.bfloat16)


def full_expert(rows, inner_own, outer_own, inner_other, outer_other):
    own = jnp.dot(gated_units(rows, inner_own), outer_own, preferred_element_type=jnp.float32)
    other = jnp.dot(gated_units(rows, inner_other), outer_other, preferred_element_type=jnp.float32)
    return (own + other).astype(jnp.bfloat16)


def on_device(
    residual,
    query_vectors,
    key_vectors,
    value_vectors,
    segment_ids,
    prompt_lengths,
    request_groups,
    page_table,
    expert_ids,
    gate_weights,
    out_weight,
    norm_gain,
    expert_inner,
    expert_outer,
):
    partner_inner = partner(expert_inner, "exp", 0)
    partner_outer = partner(expert_outer, "exp", 0)
    tok_rows, model_width = residual.shape
    req_count = lax.axis_size("req")
    member_count = lax.axis_size("exp")
    device_count = req_count * member_count
    expert_count = device_count // 2
    group_rows = tok_rows * member_count
    top_count = expert_ids.shape[1]
    capacity = 3 * tok_rows * top_count // (2 * expert_count)
    half_capacity = capacity // 2
    page_count = group_rows // PAGE
    group = lax.axis_index("req")
    member = lax.axis_index("exp")
    holds_request = (request_groups == group).astype(jnp.int32)
    my_lengths = jnp.sum(holds_request[:, None] * prompt_lengths, axis=0)
    my_pages = jnp.sum(holds_request[:, None] * page_table, axis=0)
    starts = jnp.cumsum(my_lengths) - my_lengths
    first_row = member * tok_rows
    my_segments = lax.dynamic_slice_in_dim(segment_ids, first_row, tok_rows, 0)
    prompt_index = jnp.arange(prompt_lengths.shape[1], dtype=jnp.int32)
    token_start = jnp.sum(
        jnp.where(my_segments[:, None] == prompt_index[None, :], starts[None, :], 0), axis=1
    )
    positions = (first_row + jnp.arange(tok_rows, dtype=jnp.int32) - token_start).astype(
        jnp.float32
    )
    query_turned = rotate(query_vectors, positions)
    key_turned = rotate(key_vectors, positions)
    qkv_group = lax.all_to_all(
        jnp.stack([query_turned, key_turned, value_vectors]), "exp", split_axis=2, concat_axis=1, tiled=True
    )
    query_group, key_group, value_group = qkv_group[0], qkv_group[1], qkv_group[2]
    column_count = key_group.shape[1]
    stacked = jnp.stack(
        [
            key_group.reshape(page_count, PAGE, column_count),
            value_group.reshape(page_count, PAGE, column_count),
        ],
        axis=1,
    ).reshape(page_count, -1)
    owner_of_page = my_pages // page_count
    group_range = jnp.arange(req_count, dtype=jnp.int32)
    send_select = (owner_of_page[None, :] == group_range[:, None]).astype(jnp.bfloat16)
    outgoing_pages = jnp.dot(send_select, stacked, preferred_element_type=jnp.float32).astype(
        jnp.bfloat16
    )
    incoming_pages = lax.all_to_all(outgoing_pages, "req", split_axis=0, concat_axis=0, tiled=True)
    source_holds = (request_groups[None, :] == group_range[:, None]).astype(jnp.int32)
    source_pages = jnp.sum(source_holds[:, :, None] * page_table[None, :, :], axis=1)
    slot_ids = group * page_count + jnp.arange(page_count, dtype=jnp.int32)
    place_select = jnp.sum(
        (source_pages[None, :, :] == slot_ids[:, None, None]).astype(jnp.int32), axis=2
    ).astype(jnp.bfloat16)
    kv_pages = (
        jnp.dot(place_select, incoming_pages, preferred_element_type=jnp.float32)
        .astype(jnp.bfloat16)
        .reshape(page_count, 2, PAGE, column_count)
    )
    heads_here = column_count // HEAD
    query_heads = query_group.reshape(group_rows, heads_here, HEAD)
    key_heads = key_group.reshape(group_rows, heads_here, HEAD)
    value_heads = value_group.reshape(group_rows, heads_here, HEAD)
    block_rows = min(512, group_rows)
    attended = attend_all(query_heads, key_heads, value_heads, segment_ids, block_rows)
    token_heads = lax.all_to_all(attended, "exp", split_axis=0, concat_axis=1, tiled=True)
    hidden = residual.astype(jnp.float32) + jnp.dot(
        token_heads, out_weight, preferred_element_type=jnp.float32
    )
    normed = (
        hidden * lax.rsqrt(jnp.mean(hidden * hidden, axis=-1, keepdims=True) + norm_eps) * norm_gain
    ).astype(jnp.bfloat16)
    expert_range = jnp.arange(expert_count, dtype=jnp.int32)
    chosen = (expert_ids[:, :, None] == expert_range[None, None, :]).astype(jnp.int32)
    picked = jnp.sum(chosen, axis=1)
    earlier = jnp.cumsum(picked, axis=0) - picked
    slot_rank = jnp.sum(chosen * earlier[:, None, :], axis=2)
    slot_index = expert_ids * capacity + slot_rank
    slot_range = jnp.arange(expert_count * capacity, dtype=jnp.int32)
    dispatch_matrix = jnp.sum(
        (slot_index[None, :, :] == slot_range[:, None, None]).astype(jnp.int32), axis=2
    ).astype(jnp.bfloat16)
    packed = (
        jnp.dot(dispatch_matrix, normed, preferred_element_type=jnp.float32)
        .astype(jnp.bfloat16)
        .reshape(expert_count, capacity, model_width)
    )
    outgoing = to_chunks(packed.reshape(device_count, half_capacity, model_width))
    expert_input = from_chunks(send_rows(outgoing), half_capacity, model_width)
    flat_input = expert_input.reshape(device_count * half_capacity, model_width)
    expert_out = full_expert(
        flat_input, expert_inner[0], expert_outer[0], partner_inner[0], partner_outer[0]
    ).reshape(device_count, half_capacity, model_width)
    returned = from_chunks(send_back(to_chunks(expert_out)), half_capacity, model_width).reshape(
        expert_count * capacity, model_width
    )
    combine = jnp.sum(
        jnp.where(slot_index[:, :, None] == slot_range[None, None, :], gate_weights[:, :, None], 0.0),
        axis=1,
    )
    combine_high = combine.astype(jnp.bfloat16)
    combine_low = (combine - combine_high.astype(jnp.float32)).astype(jnp.bfloat16)
    mixed = jnp.dot(combine_high, returned, preferred_element_type=jnp.float32) + jnp.dot(
        combine_low, returned, preferred_element_type=jnp.float32
    )
    layer_out = (hidden + mixed).astype(jnp.bfloat16)
    return (layer_out, kv_pages)


def solution(mesh):
    placed = (
        P(("req", "exp"), None),
        P(("req", "exp"), None),
        P(("req", "exp"), None),
        P(("req", "exp"), None),
        P("req"),
        P(),
        P(),
        P(),
        P(("req", "exp"), None),
        P(("req", "exp"), None),
        P(),
        P(),
        P(("req", "exp"), None, None),
        P(("req", "exp"), None, None),
    )
    return jax.shard_map(
        on_device,
        mesh=mesh,
        in_specs=placed,
        out_specs=(P(("req", "exp"), None), P("req", None, None, "exp")),
        check_vma=False,
    )
```

```python
import jax
import jax.numpy as jnp
from jax import lax
from jax.sharding import Mesh, PartitionSpec as P

HEAD = 128
PAGE = 128
MEMBER = ("x", "core")
EXPERT_AXES = ("req", "x")
EVERY = ("req", "x", "core")


rope_base = 10000.0
norm_eps = 1e-06
masked_score = -1e30


def partner(value, axis, distance):
    return lax.ppermute(value, axis, [(i, i ^ 1 << distance) for i in range(lax.axis_size(axis))])


def rotate(values_in, positions):
    row_count = values_in.shape[0]
    half_head = HEAD // 2
    inverse = rope_base ** (-(2.0 * jnp.arange(half_head, dtype=jnp.float32)) / HEAD)
    angles = positions[:, None] * inverse[None, :]
    cosine = jnp.cos(angles)[:, None, :]
    sines = jnp.sin(angles)[:, None, :]
    shaped = values_in.astype(jnp.float32).reshape(row_count, -1, HEAD)
    first_half = shaped[..., :half_head]
    second_half = shaped[..., half_head:]
    turned = jnp.concatenate(
        [first_half * cosine - second_half * sines, second_half * cosine + first_half * sines],
        axis=-1,
    )
    return turned.reshape(row_count, -1).astype(jnp.bfloat16)


def score_block(query_block, query_segments, key_block, key_segments):
    scores = jnp.einsum(
        "qhd,khd->hqk", query_block, key_block, preferred_element_type=jnp.float32
    ) * HEAD ** (-0.5)
    same_prompt = (query_segments[:, None] == key_segments[None, :])[None]
    return (jnp.where(same_prompt, scores, masked_score), same_prompt)


def attend_all(query_heads, key_heads, value_heads, group_segments, block_rows):
    block_count = query_heads.shape[0] // block_rows

    def one_block(block_index):
        start_row = block_index * block_rows
        query_block = lax.dynamic_slice_in_dim(query_heads, start_row, block_rows, 0)
        query_segments = lax.dynamic_slice_in_dim(group_segments, start_row, block_rows, 0)
        scores, same_prompt = score_block(query_block, query_segments, key_heads, group_segments)
        top_score = jnp.max(scores, axis=-1, keepdims=True)
        weights = jnp.where(same_prompt, jnp.exp(scores - top_score), 0.0)
        totals = jnp.sum(weights, axis=-1)
        mixed = jnp.einsum(
            "hqk,khd->qhd",
            weights.astype(jnp.bfloat16),
            value_heads,
            preferred_element_type=jnp.float32,
        )
        return (mixed / totals.T[:, :, None]).astype(jnp.bfloat16)

    results = lax.map(one_block, jnp.arange(block_count))
    return results.reshape(query_heads.shape[0], -1)


def send_rows(blocks):
    arrived = lax.all_to_all(blocks, EXPERT_AXES, split_axis=0, concat_axis=0, tiled=True)
    return arrived


def send_back(blocks):
    arrived = lax.all_to_all(blocks, EXPERT_AXES, split_axis=0, concat_axis=0, tiled=True)
    return arrived


def gated_units(rows, inner_half):
    projected = jnp.dot(rows, inner_half, preferred_element_type=jnp.float32)
    half_units = projected.shape[1] // 2
    return (jax.nn.silu(projected[:, :half_units]) * projected[:, half_units:]).astype(jnp.bfloat16)


def full_expert(rows, inner_own, outer_own, inner_other, outer_other):
    own = jnp.dot(gated_units(rows, inner_own), outer_own, preferred_element_type=jnp.float32)
    other = jnp.dot(gated_units(rows, inner_other), outer_other, preferred_element_type=jnp.float32)
    return (own + other).astype(jnp.bfloat16)


def on_device(
    residual,
    query_vectors,
    key_vectors,
    value_vectors,
    segment_ids,
    prompt_lengths,
    request_groups,
    page_table,
    expert_ids,
    gate_weights,
    out_weight,
    norm_gain,
    expert_inner,
    expert_outer,
):
    partner_inner = partner(expert_inner, "core", 0)
    partner_outer = partner(expert_outer, "core", 0)
    tok_rows, model_width = residual.shape
    req_count = lax.axis_size("req")
    member_count = lax.axis_size("x") * lax.axis_size("core")
    device_count = req_count * member_count
    expert_count = device_count // 2
    group_rows = tok_rows * member_count
    top_count = expert_ids.shape[1]
    capacity = 3 * tok_rows * top_count // (2 * expert_count)
    page_count = group_rows // PAGE
    group = lax.axis_index("req")
    member = lax.axis_index(MEMBER)
    holds_request = (request_groups == group).astype(jnp.int32)
    my_lengths = jnp.sum(holds_request[:, None] * prompt_lengths, axis=0)
    my_pages = jnp.sum(holds_request[:, None] * page_table, axis=0)
    starts = jnp.cumsum(my_lengths) - my_lengths
    first_row = member * tok_rows
    my_segments = lax.dynamic_slice_in_dim(segment_ids, first_row, tok_rows, 0)
    prompt_index = jnp.arange(prompt_lengths.shape[1], dtype=jnp.int32)
    token_start = jnp.sum(
        jnp.where(my_segments[:, None] == prompt_index[None, :], starts[None, :], 0), axis=1
    )
    positions = (first_row + jnp.arange(tok_rows, dtype=jnp.int32) - token_start).astype(
        jnp.float32
    )
    query_turned = rotate(query_vectors, positions)
    key_turned = rotate(key_vectors, positions)
    head_chunks = jnp.stack([query_turned, key_turned, value_vectors]).reshape(
        3, tok_rows, member_count, model_width // member_count
    )
    qkv_group = lax.all_to_all(
        head_chunks.transpose(0, 2, 1, 3), MEMBER, split_axis=1, concat_axis=2, tiled=True
    )
    query_group, key_group, value_group = qkv_group[0, 0], qkv_group[1, 0], qkv_group[2, 0]
    column_count = key_group.shape[1]
    stacked = jnp.stack(
        [
            key_group.reshape(page_count, PAGE, column_count),
            value_group.reshape(page_count, PAGE, column_count),
        ],
        axis=1,
    ).reshape(page_count, -1)
    owner_of_page = my_pages // page_count
    group_range = jnp.arange(req_count, dtype=jnp.int32)
    send_select = (owner_of_page[None, :] == group_range[:, None]).astype(jnp.bfloat16)
    outgoing_pages = jnp.dot(send_select, stacked, preferred_element_type=jnp.float32).astype(
        jnp.bfloat16
    )
    incoming_pages = lax.all_to_all(outgoing_pages, "req", split_axis=0, concat_axis=0, tiled=True)
    source_holds = (request_groups[None, :] == group_range[:, None]).astype(jnp.int32)
    source_pages = jnp.sum(source_holds[:, :, None] * page_table[None, :, :], axis=1)
    slot_ids = group * page_count + jnp.arange(page_count, dtype=jnp.int32)
    place_select = jnp.sum(
        (source_pages[None, :, :] == slot_ids[:, None, None]).astype(jnp.int32), axis=2
    ).astype(jnp.bfloat16)
    kv_pages = (
        jnp.dot(place_select, incoming_pages, preferred_element_type=jnp.float32)
        .astype(jnp.bfloat16)
        .reshape(page_count, 2, PAGE, column_count)
    )
    heads_here = column_count // HEAD
    query_heads = query_group.reshape(group_rows, heads_here, HEAD)
    key_heads = key_group.reshape(group_rows, heads_here, HEAD)
    value_heads = value_group.reshape(group_rows, heads_here, HEAD)
    block_rows = min(512, group_rows)
    attended = attend_all(query_heads, key_heads, value_heads, segment_ids, block_rows)
    token_heads = lax.all_to_all(attended, MEMBER, split_axis=0, concat_axis=1, tiled=True)
    hidden = residual.astype(jnp.float32) + jnp.dot(
        token_heads, out_weight, preferred_element_type=jnp.float32
    )
    normed = (
        hidden * lax.rsqrt(jnp.mean(hidden * hidden, axis=-1, keepdims=True) + norm_eps) * norm_gain
    ).astype(jnp.bfloat16)
    expert_range = jnp.arange(expert_count, dtype=jnp.int32)
    chosen = (expert_ids[:, :, None] == expert_range[None, None, :]).astype(jnp.int32)
    picked = jnp.sum(chosen, axis=1)
    earlier = jnp.cumsum(picked, axis=0) - picked
    slot_rank = jnp.sum(chosen * earlier[:, None, :], axis=2)
    slot_index = expert_ids * capacity + slot_rank
    slot_range = jnp.arange(expert_count * capacity, dtype=jnp.int32)
    dispatch_matrix = jnp.sum(
        (slot_index[None, :, :] == slot_range[:, None, None]).astype(jnp.int32), axis=2
    ).astype(jnp.bfloat16)
    packed = (
        jnp.dot(dispatch_matrix, normed, preferred_element_type=jnp.float32)
        .astype(jnp.bfloat16)
        .reshape(expert_count, capacity, model_width)
    )
    expert_input = send_rows(packed)
    flat_input = expert_input.reshape(expert_count * capacity, model_width)
    expert_out = full_expert(
        flat_input, expert_inner[0], expert_outer[0], partner_inner[0], partner_outer[0]
    ).reshape(expert_count, capacity, model_width)
    returned = send_back(expert_out).reshape(expert_count * capacity, model_width)
    combine = jnp.sum(
        jnp.where(slot_index[:, :, None] == slot_range[None, None, :], gate_weights[:, :, None], 0.0),
        axis=1,
    )
    combine_high = combine.astype(jnp.bfloat16)
    combine_low = (combine - combine_high.astype(jnp.float32)).astype(jnp.bfloat16)
    mixed = jnp.dot(combine_high, returned, preferred_element_type=jnp.float32) + jnp.dot(
        combine_low, returned, preferred_element_type=jnp.float32
    )
    layer_out = (hidden + mixed).astype(jnp.bfloat16)
    return (layer_out, kv_pages)


def solution(mesh):
    req_count, member_count = mesh.devices.shape
    fine = Mesh(mesh.devices.reshape(req_count, member_count // 2, 2), EVERY)
    token_rows = P(EVERY, None)
    placed = (
        token_rows,
        token_rows,
        token_rows,
        token_rows,
        P("req"),
        P(),
        P(),
        P(),
        token_rows,
        token_rows,
        P(),
        P(),
        P(EVERY, None, None),
        P(EVERY, None, None),
    )
    return jax.shard_map(
        on_device,
        mesh=fine,
        in_specs=placed,
        out_specs=(token_rows, P("req", None, None, MEMBER)),
        check_vma=False,
    )
```

```python
import jax
import jax.numpy as jnp
from jax import lax
from jax.sharding import Mesh, PartitionSpec as P

HEAD = 128
PAGE = 128
MEMBER = ("x", "core")
EXPERT_AXES = ("req", "x")
EVERY = ("req", "x", "core")


rope_base = 10000.0
norm_eps = 1e-06
masked_score = -1e30


def partner(value, axis, distance):
    return lax.ppermute(value, axis, [(i, i ^ 1 << distance) for i in range(lax.axis_size(axis))])


def rotate(values_in, positions):
    row_count = values_in.shape[0]
    half_head = HEAD // 2
    inverse = rope_base ** (-(2.0 * jnp.arange(half_head, dtype=jnp.float32)) / HEAD)
    angles = positions[:, None] * inverse[None, :]
    cosine = jnp.cos(angles)[:, None, :]
    sines = jnp.sin(angles)[:, None, :]
    shaped = values_in.astype(jnp.float32).reshape(row_count, -1, HEAD)
    first_half = shaped[..., :half_head]
    second_half = shaped[..., half_head:]
    turned = jnp.concatenate(
        [first_half * cosine - second_half * sines, second_half * cosine + first_half * sines],
        axis=-1,
    )
    return turned.reshape(row_count, -1).astype(jnp.bfloat16)


def score_block(query_block, query_segments, key_block, key_segments):
    scores = jnp.einsum(
        "qhd,khd->hqk", query_block, key_block, preferred_element_type=jnp.float32
    ) * HEAD ** (-0.5)
    same_prompt = (query_segments[:, None] == key_segments[None, :])[None]
    return (jnp.where(same_prompt, scores, masked_score), same_prompt)


def attend_all(query_heads, key_heads, value_heads, group_segments, block_rows):
    block_count = query_heads.shape[0] // block_rows

    def one_block(block_index):
        start_row = block_index * block_rows
        query_block = lax.dynamic_slice_in_dim(query_heads, start_row, block_rows, 0)
        query_segments = lax.dynamic_slice_in_dim(group_segments, start_row, block_rows, 0)
        scores, same_prompt = score_block(query_block, query_segments, key_heads, group_segments)
        top_score = jnp.max(scores, axis=-1, keepdims=True)
        weights = jnp.where(same_prompt, jnp.exp(scores - top_score), 0.0)
        totals = jnp.sum(weights, axis=-1)
        mixed = jnp.einsum(
            "hqk,khd->qhd",
            weights.astype(jnp.bfloat16),
            value_heads,
            preferred_element_type=jnp.float32,
        )
        return (mixed / totals.T[:, :, None]).astype(jnp.bfloat16)

    results = lax.map(one_block, jnp.arange(block_count))
    return results.reshape(query_heads.shape[0], -1)


def send_rows(blocks):
    arrived = lax.all_to_all(blocks, EXPERT_AXES, split_axis=0, concat_axis=0, tiled=True)
    return arrived


def send_back(blocks):
    arrived = lax.all_to_all(blocks, EXPERT_AXES, split_axis=0, concat_axis=0, tiled=True)
    return arrived


def full_expert(rows, inner_both, outer_both):
    projected = jnp.dot(rows, inner_both, preferred_element_type=jnp.float32)
    quarter = projected.shape[1] // 4
    active = jnp.concatenate(
        [
            jax.nn.silu(projected[:, :quarter]) * projected[:, quarter : 2 * quarter],
            jax.nn.silu(projected[:, 2 * quarter : 3 * quarter]) * projected[:, 3 * quarter :],
        ],
        axis=1,
    ).astype(jnp.bfloat16)
    return jnp.dot(active, outer_both, preferred_element_type=jnp.float32).astype(jnp.bfloat16)


def on_device(
    residual,
    query_vectors,
    key_vectors,
    value_vectors,
    segment_ids,
    prompt_lengths,
    request_groups,
    page_table,
    expert_ids,
    gate_weights,
    out_weight,
    norm_gain,
    expert_inner,
    expert_outer,
):
    partner_inner = partner(expert_inner, "core", 0)
    partner_outer = partner(expert_outer, "core", 0)
    tok_rows, model_width = residual.shape
    req_count = lax.axis_size("req")
    member_count = lax.axis_size("x") * lax.axis_size("core")
    device_count = req_count * member_count
    expert_count = device_count // 2
    group_rows = tok_rows * member_count
    top_count = expert_ids.shape[1]
    capacity = 3 * tok_rows * top_count // (2 * expert_count)
    page_count = group_rows // PAGE
    group = lax.axis_index("req")
    member = lax.axis_index(MEMBER)
    holds_request = (request_groups == group).astype(jnp.int32)
    my_lengths = jnp.sum(holds_request[:, None] * prompt_lengths, axis=0)
    my_pages = jnp.sum(holds_request[:, None] * page_table, axis=0)
    starts = jnp.cumsum(my_lengths) - my_lengths
    first_row = member * tok_rows
    my_segments = lax.dynamic_slice_in_dim(segment_ids, first_row, tok_rows, 0)
    prompt_index = jnp.arange(prompt_lengths.shape[1], dtype=jnp.int32)
    token_start = jnp.sum(
        jnp.where(my_segments[:, None] == prompt_index[None, :], starts[None, :], 0), axis=1
    )
    positions = (first_row + jnp.arange(tok_rows, dtype=jnp.int32) - token_start).astype(
        jnp.float32
    )
    query_turned = rotate(query_vectors, positions)
    key_turned = rotate(key_vectors, positions)
    head_chunks = jnp.stack([query_turned, key_turned, value_vectors]).reshape(
        3, tok_rows, member_count, model_width // member_count
    )
    qkv_group = lax.all_to_all(
        head_chunks.transpose(0, 2, 1, 3), MEMBER, split_axis=1, concat_axis=2, tiled=True
    )
    query_group, key_group, value_group = qkv_group[0, 0], qkv_group[1, 0], qkv_group[2, 0]
    column_count = key_group.shape[1]
    stacked = jnp.stack(
        [
            key_group.reshape(page_count, PAGE, column_count),
            value_group.reshape(page_count, PAGE, column_count),
        ],
        axis=1,
    ).reshape(page_count, -1)
    owner_of_page = my_pages // page_count
    group_range = jnp.arange(req_count, dtype=jnp.int32)
    send_select = (owner_of_page[None, :] == group_range[:, None]).astype(jnp.bfloat16)
    outgoing_pages = jnp.dot(send_select, stacked, preferred_element_type=jnp.float32).astype(
        jnp.bfloat16
    )
    incoming_pages = lax.all_to_all(outgoing_pages, "req", split_axis=0, concat_axis=0, tiled=True)
    source_holds = (request_groups[None, :] == group_range[:, None]).astype(jnp.int32)
    source_pages = jnp.sum(source_holds[:, :, None] * page_table[None, :, :], axis=1)
    slot_ids = group * page_count + jnp.arange(page_count, dtype=jnp.int32)
    place_select = jnp.sum(
        (source_pages[None, :, :] == slot_ids[:, None, None]).astype(jnp.int32), axis=2
    ).astype(jnp.bfloat16)
    kv_pages = (
        jnp.dot(place_select, incoming_pages, preferred_element_type=jnp.float32)
        .astype(jnp.bfloat16)
        .reshape(page_count, 2, PAGE, column_count)
    )
    heads_here = column_count // HEAD
    query_heads = query_group.reshape(group_rows, heads_here, HEAD)
    key_heads = key_group.reshape(group_rows, heads_here, HEAD)
    value_heads = value_group.reshape(group_rows, heads_here, HEAD)
    block_rows = min(512, group_rows)
    attended = attend_all(query_heads, key_heads, value_heads, segment_ids, block_rows)
    token_heads = lax.all_to_all(attended, MEMBER, split_axis=0, concat_axis=1, tiled=True)
    hidden = residual.astype(jnp.float32) + jnp.dot(
        token_heads, out_weight, preferred_element_type=jnp.float32
    )
    normed = (
        hidden * lax.rsqrt(jnp.mean(hidden * hidden, axis=-1, keepdims=True) + norm_eps) * norm_gain
    ).astype(jnp.bfloat16)
    expert_range = jnp.arange(expert_count, dtype=jnp.int32)
    chosen = (expert_ids[:, :, None] == expert_range[None, None, :]).astype(jnp.int32)
    picked = jnp.sum(chosen, axis=1)
    earlier = jnp.cumsum(picked, axis=0) - picked
    slot_rank = jnp.sum(chosen * earlier[:, None, :], axis=2)
    slot_index = expert_ids * capacity + slot_rank
    slot_range = jnp.arange(expert_count * capacity, dtype=jnp.int32)
    dispatch_matrix = jnp.sum(
        (slot_index[None, :, :] == slot_range[:, None, None]).astype(jnp.int32), axis=2
    ).astype(jnp.bfloat16)
    combine = jnp.sum(
        jnp.where(slot_index[:, :, None] == slot_range[None, None, :], gate_weights[:, :, None], 0.0),
        axis=1,
    )
    combine_high = combine.astype(jnp.bfloat16)
    combine_low = (combine - combine_high.astype(jnp.float32)).astype(jnp.bfloat16)
    inner_both = jnp.concatenate([expert_inner[0], partner_inner[0]], axis=1)
    outer_both = jnp.concatenate([expert_outer[0], partner_outer[0]], axis=0)
    chunk_rows = 8
    chunk_count = capacity // chunk_rows
    dispatch_chunks = dispatch_matrix.reshape(expert_count, chunk_count, chunk_rows, tok_rows)
    high_chunks = combine_high.reshape(tok_rows, expert_count, chunk_count, chunk_rows)
    low_chunks = combine_low.reshape(tok_rows, expert_count, chunk_count, chunk_rows)
    mixed = jnp.zeros((tok_rows, model_width), jnp.float32)
    for chunk in range(chunk_count):
        chunk_select = dispatch_chunks[:, chunk].reshape(expert_count * chunk_rows, tok_rows)
        packed = jnp.dot(chunk_select, normed, preferred_element_type=jnp.float32).astype(jnp.bfloat16)
        expert_input = send_rows(packed.reshape(expert_count, chunk_rows, model_width))
        expert_out = full_expert(
            expert_input.reshape(expert_count * chunk_rows, model_width), inner_both, outer_both
        )
        returned = send_back(expert_out.reshape(expert_count, chunk_rows, model_width)).reshape(
            expert_count * chunk_rows, model_width
        )
        high = high_chunks[:, :, chunk].reshape(tok_rows, expert_count * chunk_rows)
        low = low_chunks[:, :, chunk].reshape(tok_rows, expert_count * chunk_rows)
        mixed = mixed + (
            jnp.dot(high, returned, preferred_element_type=jnp.float32)
            + jnp.dot(low, returned, preferred_element_type=jnp.float32)
        )
    layer_out = (hidden + mixed).astype(jnp.bfloat16)
    return (layer_out, kv_pages)


def solution(mesh):
    req_count, member_count = mesh.devices.shape
    fine = Mesh(mesh.devices.reshape(req_count, member_count // 2, 2), EVERY)
    token_rows = P(EVERY, None)
    placed = (
        token_rows,
        token_rows,
        token_rows,
        token_rows,
        P("req"),
        P(),
        P(),
        P(),
        token_rows,
        token_rows,
        P(),
        P(),
        P(EVERY, None, None),
        P(EVERY, None, None),
    )
    return jax.shard_map(
        on_device,
        mesh=fine,
        in_specs=placed,
        out_specs=(token_rows, P("req", None, None, MEMBER)),
        check_vma=False,
    )
```

```python
import jax
import jax.numpy as jnp
from jax import lax
from jax.sharding import Mesh, PartitionSpec as P

HEAD = 128
PAGE = 128
MEMBER = ("x", "core")
EXPERT_AXES = ("req", "x")
EVERY = ("req", "x", "core")


rope_base = 10000.0
norm_eps = 1e-06
masked_score = -1e30


def partner(value, axis, distance):
    return lax.ppermute(value, axis, [(i, i ^ 1 << distance) for i in range(lax.axis_size(axis))])


def rotate(values_in, positions):
    row_count = values_in.shape[0]
    half_head = HEAD // 2
    inverse = rope_base ** (-(2.0 * jnp.arange(half_head, dtype=jnp.float32)) / HEAD)
    angles = positions[:, None] * inverse[None, :]
    cosine = jnp.cos(angles)[:, None, :]
    sines = jnp.sin(angles)[:, None, :]
    shaped = values_in.astype(jnp.float32).reshape(row_count, -1, HEAD)
    first_half = shaped[..., :half_head]
    second_half = shaped[..., half_head:]
    turned = jnp.concatenate(
        [first_half * cosine - second_half * sines, second_half * cosine + first_half * sines],
        axis=-1,
    )
    return turned.reshape(row_count, -1).astype(jnp.bfloat16)


def score_block(query_block, query_segments, key_block, key_segments):
    scores = jnp.einsum(
        "qhd,khd->hqk", query_block, key_block, preferred_element_type=jnp.float32
    ) * HEAD ** (-0.5)
    same_prompt = (query_segments[:, None] == key_segments[None, :])[None]
    return (jnp.where(same_prompt, scores, masked_score), same_prompt)


def attend_all(query_heads, key_heads, value_heads, group_segments, block_rows):
    block_count = query_heads.shape[0] // block_rows

    def one_block(block_index):
        start_row = block_index * block_rows
        query_block = lax.dynamic_slice_in_dim(query_heads, start_row, block_rows, 0)
        query_segments = lax.dynamic_slice_in_dim(group_segments, start_row, block_rows, 0)
        scores, same_prompt = score_block(query_block, query_segments, key_heads, group_segments)
        top_score = jnp.max(scores, axis=-1, keepdims=True)
        weights = jnp.where(same_prompt, jnp.exp(scores - top_score), 0.0)
        totals = jnp.sum(weights, axis=-1)
        mixed = jnp.einsum(
            "hqk,khd->qhd",
            weights.astype(jnp.bfloat16),
            value_heads,
            preferred_element_type=jnp.float32,
        )
        return (mixed / totals.T[:, :, None]).astype(jnp.bfloat16)

    results = lax.map(one_block, jnp.arange(block_count))
    return results.reshape(query_heads.shape[0], -1)


def send_rows(blocks):
    arrived = lax.all_to_all(blocks, EXPERT_AXES, split_axis=0, concat_axis=0, tiled=True)
    return arrived


def send_back(blocks):
    arrived = lax.all_to_all(blocks, EXPERT_AXES, split_axis=0, concat_axis=0, tiled=True)
    return arrived


def gated_units(rows, inner_half):
    projected = jnp.dot(rows, inner_half, preferred_element_type=jnp.float32)
    half_units = projected.shape[1] // 2
    return (jax.nn.silu(projected[:, :half_units]) * projected[:, half_units:]).astype(jnp.bfloat16)


def full_expert(rows, inner_own, outer_own, inner_other, outer_other):
    own = jnp.dot(gated_units(rows, inner_own), outer_own, preferred_element_type=jnp.float32)
    other = jnp.dot(gated_units(rows, inner_other), outer_other, preferred_element_type=jnp.float32)
    return (own + other).astype(jnp.bfloat16)


def on_device(
    residual,
    query_vectors,
    key_vectors,
    value_vectors,
    segment_ids,
    prompt_lengths,
    request_groups,
    page_table,
    expert_ids,
    gate_weights,
    out_weight,
    norm_gain,
    expert_inner,
    expert_outer,
):
    partner_inner = partner(expert_inner, "core", 0)
    partner_outer = partner(expert_outer, "core", 0)
    tok_rows, model_width = residual.shape
    req_count = lax.axis_size("req")
    member_count = lax.axis_size("x") * lax.axis_size("core")
    device_count = req_count * member_count
    expert_count = device_count // 2
    group_rows = tok_rows * member_count
    top_count = expert_ids.shape[1]
    capacity = 3 * tok_rows * top_count // (2 * expert_count)
    page_count = group_rows // PAGE
    group = lax.axis_index("req")
    member = lax.axis_index(MEMBER)
    holds_request = (request_groups == group).astype(jnp.int32)
    my_lengths = jnp.sum(holds_request[:, None] * prompt_lengths, axis=0)
    my_pages = jnp.sum(holds_request[:, None] * page_table, axis=0)
    starts = jnp.cumsum(my_lengths) - my_lengths
    first_row = member * tok_rows
    my_segments = lax.dynamic_slice_in_dim(segment_ids, first_row, tok_rows, 0)
    prompt_index = jnp.arange(prompt_lengths.shape[1], dtype=jnp.int32)
    token_start = jnp.sum(
        jnp.where(my_segments[:, None] == prompt_index[None, :], starts[None, :], 0), axis=1
    )
    positions = (first_row + jnp.arange(tok_rows, dtype=jnp.int32) - token_start).astype(
        jnp.float32
    )
    query_turned = rotate(query_vectors, positions)
    key_turned = rotate(key_vectors, positions)
    head_chunks = jnp.stack([query_turned, key_turned, value_vectors]).reshape(
        3, tok_rows, member_count, model_width // member_count
    )
    qkv_group = lax.all_to_all(
        head_chunks.transpose(0, 2, 1, 3), MEMBER, split_axis=1, concat_axis=2, tiled=True
    )
    query_group, key_group, value_group = qkv_group[0, 0], qkv_group[1, 0], qkv_group[2, 0]
    column_count = key_group.shape[1]
    stacked = jnp.stack(
        [
            key_group.reshape(page_count, PAGE, column_count),
            value_group.reshape(page_count, PAGE, column_count),
        ],
        axis=1,
    ).reshape(page_count, -1)
    owner_of_page = my_pages // page_count
    group_range = jnp.arange(req_count, dtype=jnp.int32)
    send_select = (owner_of_page[None, :] == group_range[:, None]).astype(jnp.bfloat16)
    outgoing_pages = jnp.dot(send_select, stacked, preferred_element_type=jnp.float32).astype(
        jnp.bfloat16
    )
    incoming_pages = lax.all_to_all(outgoing_pages, "req", split_axis=0, concat_axis=0, tiled=True)
    source_holds = (request_groups[None, :] == group_range[:, None]).astype(jnp.int32)
    source_pages = jnp.sum(source_holds[:, :, None] * page_table[None, :, :], axis=1)
    slot_ids = group * page_count + jnp.arange(page_count, dtype=jnp.int32)
    place_select = jnp.sum(
        (source_pages[None, :, :] == slot_ids[:, None, None]).astype(jnp.int32), axis=2
    ).astype(jnp.bfloat16)
    kv_pages = (
        jnp.dot(place_select, incoming_pages, preferred_element_type=jnp.float32)
        .astype(jnp.bfloat16)
        .reshape(page_count, 2, PAGE, column_count)
    )
    heads_here = column_count // HEAD
    query_heads = query_group.reshape(group_rows, heads_here, HEAD)
    key_heads = key_group.reshape(group_rows, heads_here, HEAD)
    value_heads = value_group.reshape(group_rows, heads_here, HEAD)
    block_rows = min(512, group_rows)
    attended = attend_all(query_heads, key_heads, value_heads, segment_ids, block_rows)
    token_heads = lax.all_to_all(attended, MEMBER, split_axis=0, concat_axis=1, tiled=True)
    hidden = residual.astype(jnp.float32) + jnp.dot(
        token_heads, out_weight, preferred_element_type=jnp.float32
    )
    normed = (
        hidden * lax.rsqrt(jnp.mean(hidden * hidden, axis=-1, keepdims=True) + norm_eps) * norm_gain
    ).astype(jnp.bfloat16)
    expert_range = jnp.arange(expert_count, dtype=jnp.int32)
    chosen = (expert_ids[:, :, None] == expert_range[None, None, :]).astype(jnp.int32)
    picked = jnp.sum(chosen, axis=1)
    earlier = jnp.cumsum(picked, axis=0) - picked
    slot_rank = jnp.sum(chosen * earlier[:, None, :], axis=2)
    slot_index = expert_ids * capacity + slot_rank
    slot_range = jnp.arange(expert_count * capacity, dtype=jnp.int32)
    dispatch_matrix = jnp.sum(
        (slot_index[None, :, :] == slot_range[:, None, None]).astype(jnp.int32), axis=2
    ).astype(jnp.bfloat16)
    combine = jnp.sum(
        jnp.where(slot_index[:, :, None] == slot_range[None, None, :], gate_weights[:, :, None], 0.0),
        axis=1,
    )
    combine_high = combine.astype(jnp.bfloat16).reshape(tok_rows, expert_count, capacity)
    combine_low = (combine - combine_high.reshape(tok_rows, -1).astype(jnp.float32)).astype(
        jnp.bfloat16
    ).reshape(tok_rows, expert_count, capacity)
    dispatch_slots = dispatch_matrix.reshape(expert_count, capacity, tok_rows)
    first_rows = 2 * capacity // 3
    mixed = jnp.zeros((tok_rows, model_width), jnp.float32)
    for low_slot, high_slot in ((0, first_rows), (first_rows, capacity)):
        chunk_rows = high_slot - low_slot
        chunk_select = dispatch_slots[:, low_slot:high_slot].reshape(expert_count * chunk_rows, tok_rows)
        packed = jnp.dot(chunk_select, normed, preferred_element_type=jnp.float32).astype(jnp.bfloat16)
        expert_input = send_rows(packed.reshape(expert_count, chunk_rows, model_width))
        expert_out = full_expert(
            expert_input.reshape(expert_count * chunk_rows, model_width),
            expert_inner[0],
            expert_outer[0],
            partner_inner[0],
            partner_outer[0],
        )
        returned = send_back(expert_out.reshape(expert_count, chunk_rows, model_width)).reshape(
            expert_count * chunk_rows, model_width
        )
        high = combine_high[:, :, low_slot:high_slot].reshape(tok_rows, expert_count * chunk_rows)
        low = combine_low[:, :, low_slot:high_slot].reshape(tok_rows, expert_count * chunk_rows)
        mixed = mixed + (
            jnp.dot(high, returned, preferred_element_type=jnp.float32)
            + jnp.dot(low, returned, preferred_element_type=jnp.float32)
        )
    layer_out = (hidden + mixed).astype(jnp.bfloat16)
    return (layer_out, kv_pages)


def solution(mesh):
    req_count, member_count = mesh.devices.shape
    fine = Mesh(mesh.devices.reshape(req_count, member_count // 2, 2), EVERY)
    token_rows = P(EVERY, None)
    placed = (
        token_rows,
        token_rows,
        token_rows,
        token_rows,
        P("req"),
        P(),
        P(),
        P(),
        token_rows,
        token_rows,
        P(),
        P(),
        P(EVERY, None, None),
        P(EVERY, None, None),
    )
    return jax.shard_map(
        on_device,
        mesh=fine,
        in_specs=placed,
        out_specs=(token_rows, P("req", None, None, MEMBER)),
        check_vma=False,
    )
```

```python
import jax
import jax.numpy as jnp
from jax import lax
from jax.sharding import Mesh, PartitionSpec as P

HEAD = 128
PAGE = 128
MEMBER = ("x", "core")
EXPERT_AXES = ("req", "x")
EVERY = ("req", "x", "core")


rope_base = 10000.0
norm_eps = 1e-06
masked_score = -1e30


def partner(value, axis, distance):
    return lax.ppermute(value, axis, [(i, i ^ 1 << distance) for i in range(lax.axis_size(axis))])


def rotate(values_in, positions):
    row_count = values_in.shape[0]
    half_head = HEAD // 2
    inverse = rope_base ** (-(2.0 * jnp.arange(half_head, dtype=jnp.float32)) / HEAD)
    angles = positions[:, None] * inverse[None, :]
    cosine = jnp.cos(angles)[:, None, :]
    sines = jnp.sin(angles)[:, None, :]
    shaped = values_in.astype(jnp.float32).reshape(row_count, -1, HEAD)
    first_half = shaped[..., :half_head]
    second_half = shaped[..., half_head:]
    turned = jnp.concatenate(
        [first_half * cosine - second_half * sines, second_half * cosine + first_half * sines],
        axis=-1,
    )
    return turned.reshape(row_count, -1).astype(jnp.bfloat16)


def score_block(query_block, query_segments, key_block, key_segments):
    scores = jnp.einsum(
        "qhd,khd->hqk", query_block, key_block, preferred_element_type=jnp.float32
    ) * HEAD ** (-0.5)
    same_prompt = (query_segments[:, None] == key_segments[None, :])[None]
    return (jnp.where(same_prompt, scores, masked_score), same_prompt)


def attend_all(query_heads, key_heads, value_heads, group_segments, block_rows):
    block_count = query_heads.shape[0] // block_rows

    def one_block(block_index):
        start_row = block_index * block_rows
        query_block = lax.dynamic_slice_in_dim(query_heads, start_row, block_rows, 0)
        query_segments = lax.dynamic_slice_in_dim(group_segments, start_row, block_rows, 0)
        scores, same_prompt = score_block(query_block, query_segments, key_heads, group_segments)
        top_score = jnp.max(scores, axis=-1, keepdims=True)
        weights = jnp.where(same_prompt, jnp.exp(scores - top_score), 0.0)
        totals = jnp.sum(weights, axis=-1)
        mixed = jnp.einsum(
            "hqk,khd->qhd",
            weights.astype(jnp.bfloat16),
            value_heads,
            preferred_element_type=jnp.float32,
        )
        return (mixed / totals.T[:, :, None]).astype(jnp.bfloat16)

    results = lax.map(one_block, jnp.arange(block_count))
    return results.reshape(query_heads.shape[0], -1)


def send_rows(blocks):
    arrived = lax.all_to_all(blocks, EXPERT_AXES, split_axis=0, concat_axis=0, tiled=True)
    return arrived


def send_back(blocks):
    arrived = lax.all_to_all(blocks, EXPERT_AXES, split_axis=0, concat_axis=0, tiled=True)
    return arrived


def full_expert(rows, inner_both, outer_both):
    projected = jnp.dot(rows, inner_both, preferred_element_type=jnp.float32)
    quarter = projected.shape[1] // 4
    active = jnp.concatenate(
        [
            jax.nn.silu(projected[:, :quarter]) * projected[:, quarter : 2 * quarter],
            jax.nn.silu(projected[:, 2 * quarter : 3 * quarter]) * projected[:, 3 * quarter :],
        ],
        axis=1,
    ).astype(jnp.bfloat16)
    return jnp.dot(active, outer_both, preferred_element_type=jnp.float32).astype(jnp.bfloat16)


def on_device(
    residual,
    query_vectors,
    key_vectors,
    value_vectors,
    segment_ids,
    prompt_lengths,
    request_groups,
    page_table,
    expert_ids,
    gate_weights,
    out_weight,
    norm_gain,
    expert_inner,
    expert_outer,
):
    partner_inner = partner(expert_inner, "core", 0)
    partner_outer = partner(expert_outer, "core", 0)
    tok_rows, model_width = residual.shape
    req_count = lax.axis_size("req")
    member_count = lax.axis_size("x") * lax.axis_size("core")
    device_count = req_count * member_count
    expert_count = device_count // 2
    group_rows = tok_rows * member_count
    top_count = expert_ids.shape[1]
    capacity = 3 * tok_rows * top_count // (2 * expert_count)
    page_count = group_rows // PAGE
    group = lax.axis_index("req")
    member = lax.axis_index(MEMBER)
    holds_request = (request_groups == group).astype(jnp.int32)
    my_lengths = jnp.sum(holds_request[:, None] * prompt_lengths, axis=0)
    my_pages = jnp.sum(holds_request[:, None] * page_table, axis=0)
    starts = jnp.cumsum(my_lengths) - my_lengths
    first_row = member * tok_rows
    my_segments = lax.dynamic_slice_in_dim(segment_ids, first_row, tok_rows, 0)
    prompt_index = jnp.arange(prompt_lengths.shape[1], dtype=jnp.int32)
    token_start = jnp.sum(
        jnp.where(my_segments[:, None] == prompt_index[None, :], starts[None, :], 0), axis=1
    )
    positions = (first_row + jnp.arange(tok_rows, dtype=jnp.int32) - token_start).astype(
        jnp.float32
    )
    query_turned = rotate(query_vectors, positions)
    key_turned = rotate(key_vectors, positions)
    head_chunks = jnp.stack([query_turned, key_turned, value_vectors]).reshape(
        3, tok_rows, member_count, model_width // member_count
    )
    qkv_group = lax.all_to_all(
        head_chunks.transpose(0, 2, 1, 3), MEMBER, split_axis=1, concat_axis=2, tiled=True
    )
    query_group, key_group, value_group = qkv_group[0, 0], qkv_group[1, 0], qkv_group[2, 0]
    column_count = key_group.shape[1]
    stacked = jnp.stack(
        [
            key_group.reshape(page_count, PAGE, column_count),
            value_group.reshape(page_count, PAGE, column_count),
        ],
        axis=1,
    ).reshape(page_count, -1)
    owner_of_page = my_pages // page_count
    group_range = jnp.arange(req_count, dtype=jnp.int32)
    send_select = (owner_of_page[None, :] == group_range[:, None]).astype(jnp.bfloat16)
    outgoing_pages = jnp.dot(send_select, stacked, preferred_element_type=jnp.float32).astype(
        jnp.bfloat16
    )
    incoming_pages = lax.all_to_all(outgoing_pages, "req", split_axis=0, concat_axis=0, tiled=True)
    source_holds = (request_groups[None, :] == group_range[:, None]).astype(jnp.int32)
    source_pages = jnp.sum(source_holds[:, :, None] * page_table[None, :, :], axis=1)
    slot_ids = group * page_count + jnp.arange(page_count, dtype=jnp.int32)
    place_select = jnp.sum(
        (source_pages[None, :, :] == slot_ids[:, None, None]).astype(jnp.int32), axis=2
    ).astype(jnp.bfloat16)
    kv_pages = (
        jnp.dot(place_select, incoming_pages, preferred_element_type=jnp.float32)
        .astype(jnp.bfloat16)
        .reshape(page_count, 2, PAGE, column_count)
    )
    heads_here = column_count // HEAD
    query_heads = query_group.reshape(group_rows, heads_here, HEAD)
    key_heads = key_group.reshape(group_rows, heads_here, HEAD)
    value_heads = value_group.reshape(group_rows, heads_here, HEAD)
    block_rows = group_rows
    attended = attend_all(query_heads, key_heads, value_heads, segment_ids, block_rows)
    token_heads = lax.all_to_all(attended, MEMBER, split_axis=0, concat_axis=1, tiled=True)
    hidden = residual.astype(jnp.float32) + jnp.dot(
        token_heads, out_weight, preferred_element_type=jnp.float32
    )
    normed = (
        hidden * lax.rsqrt(jnp.mean(hidden * hidden, axis=-1, keepdims=True) + norm_eps) * norm_gain
    ).astype(jnp.bfloat16)
    expert_range = jnp.arange(expert_count, dtype=jnp.int32)
    chosen = (expert_ids[:, :, None] == expert_range[None, None, :]).astype(jnp.int32)
    picked = jnp.sum(chosen, axis=1)
    earlier = jnp.cumsum(picked, axis=0) - picked
    slot_rank = jnp.sum(chosen * earlier[:, None, :], axis=2)
    slot_index = expert_ids * capacity + slot_rank
    slot_range = jnp.arange(expert_count * capacity, dtype=jnp.int32)
    dispatch_matrix = jnp.sum(
        (slot_index[None, :, :] == slot_range[:, None, None]).astype(jnp.int32), axis=2
    ).astype(jnp.bfloat16)
    packed = (
        jnp.dot(dispatch_matrix, normed, preferred_element_type=jnp.float32)
        .astype(jnp.bfloat16)
        .reshape(expert_count, capacity, model_width)
    )
    expert_input = send_rows(packed)
    flat_input = expert_input.reshape(expert_count * capacity, model_width)
    inner_both = jnp.concatenate([expert_inner[0], partner_inner[0]], axis=1)
    outer_both = jnp.concatenate([expert_outer[0], partner_outer[0]], axis=0)
    expert_out = full_expert(flat_input, inner_both, outer_both).reshape(
        expert_count, capacity, model_width
    )
    returned = send_back(expert_out).reshape(expert_count * capacity, model_width)
    combine = jnp.sum(
        jnp.where(slot_index[:, :, None] == slot_range[None, None, :], gate_weights[:, :, None], 0.0),
        axis=1,
    )
    combine_high = combine.astype(jnp.bfloat16)
    combine_low = (combine - combine_high.astype(jnp.float32)).astype(jnp.bfloat16)
    both_parts = jnp.dot(
        jnp.concatenate([combine_high, combine_low], axis=0), returned, preferred_element_type=jnp.float32
    )
    mixed = both_parts[:tok_rows] + both_parts[tok_rows:]
    layer_out = (hidden + mixed).astype(jnp.bfloat16)
    return (layer_out, kv_pages)


def solution(mesh):
    req_count, member_count = mesh.devices.shape
    fine = Mesh(mesh.devices.reshape(req_count, member_count // 2, 2), EVERY)
    token_rows = P(EVERY, None)
    placed = (
        token_rows,
        token_rows,
        token_rows,
        token_rows,
        P("req"),
        P(),
        P(),
        P(),
        token_rows,
        token_rows,
        P(),
        P(),
        P(EVERY, None, None),
        P(EVERY, None, None),
    )
    return jax.shard_map(
        on_device,
        mesh=fine,
        in_specs=placed,
        out_specs=(token_rows, P("req", None, None, MEMBER)),
        check_vma=False,
    )
```

```python
import jax
import jax.numpy as jnp
from jax import lax
from jax.sharding import Mesh, PartitionSpec as P

HEAD = 128
PAGE = 128
MEMBER = ("x", "core")
EXPERT_AXES = ("req", "x")
EVERY = ("req", "x", "core")


rope_base = 10000.0
norm_eps = 1e-06
masked_score = -1e30


def partner(value, axis, distance):
    return lax.ppermute(value, axis, [(i, i ^ 1 << distance) for i in range(lax.axis_size(axis))])


def rotate(values_in, positions):
    row_count = values_in.shape[0]
    half_head = HEAD // 2
    inverse = rope_base ** (-(2.0 * jnp.arange(half_head, dtype=jnp.float32)) / HEAD)
    angles = positions[:, None] * inverse[None, :]
    cosine = jnp.cos(angles)[:, None, :]
    sines = jnp.sin(angles)[:, None, :]
    shaped = values_in.astype(jnp.float32).reshape(row_count, -1, HEAD)
    first_half = shaped[..., :half_head]
    second_half = shaped[..., half_head:]
    turned = jnp.concatenate(
        [first_half * cosine - second_half * sines, second_half * cosine + first_half * sines],
        axis=-1,
    )
    return turned.reshape(row_count, -1).astype(jnp.bfloat16)


def score_block(query_block, query_segments, key_block, key_segments):
    scores = jnp.einsum(
        "qhd,khd->hqk", query_block, key_block, preferred_element_type=jnp.float32
    ) * HEAD ** (-0.5)
    same_prompt = (query_segments[:, None] == key_segments[None, :])[None]
    return (jnp.where(same_prompt, scores, masked_score), same_prompt)


def attend_all(query_heads, key_heads, value_heads, group_segments, block_rows):
    block_count = query_heads.shape[0] // block_rows

    def one_block(block_index):
        start_row = block_index * block_rows
        query_block = lax.dynamic_slice_in_dim(query_heads, start_row, block_rows, 0)
        query_segments = lax.dynamic_slice_in_dim(group_segments, start_row, block_rows, 0)
        scores, same_prompt = score_block(query_block, query_segments, key_heads, group_segments)
        top_score = jnp.max(scores, axis=-1, keepdims=True)
        weights = jnp.where(same_prompt, jnp.exp(scores - top_score), 0.0)
        totals = jnp.sum(weights, axis=-1)
        mixed = jnp.einsum(
            "hqk,khd->qhd",
            weights.astype(jnp.bfloat16),
            value_heads,
            preferred_element_type=jnp.float32,
        )
        return (mixed / totals.T[:, :, None]).astype(jnp.bfloat16)

    results = lax.map(one_block, jnp.arange(block_count))
    return results.reshape(query_heads.shape[0], -1)


def send_rows(blocks):
    arrived = lax.all_to_all(blocks, EXPERT_AXES, split_axis=0, concat_axis=0, tiled=True)
    return arrived


def send_back(blocks):
    arrived = lax.all_to_all(blocks, EXPERT_AXES, split_axis=0, concat_axis=0, tiled=True)
    return arrived


def full_expert(rows, inner_both, outer_both):
    projected = jnp.dot(rows, inner_both, preferred_element_type=jnp.float32)
    quarter = projected.shape[1] // 4
    active = jnp.concatenate(
        [
            jax.nn.silu(projected[:, :quarter]) * projected[:, quarter : 2 * quarter],
            jax.nn.silu(projected[:, 2 * quarter : 3 * quarter]) * projected[:, 3 * quarter :],
        ],
        axis=1,
    ).astype(jnp.bfloat16)
    return jnp.dot(active, outer_both, preferred_element_type=jnp.float32).astype(jnp.bfloat16)


def on_device(
    residual,
    query_vectors,
    key_vectors,
    value_vectors,
    segment_ids,
    prompt_lengths,
    request_groups,
    page_table,
    expert_ids,
    gate_weights,
    out_weight,
    norm_gain,
    expert_inner,
    expert_outer,
):
    partner_inner = partner(expert_inner, "core", 0)
    partner_outer = partner(expert_outer, "core", 0)
    tok_rows, model_width = residual.shape
    req_count = lax.axis_size("req")
    member_count = lax.axis_size("x") * lax.axis_size("core")
    device_count = req_count * member_count
    expert_count = device_count // 2
    group_rows = tok_rows * member_count
    top_count = expert_ids.shape[1]
    capacity = 3 * tok_rows * top_count // (2 * expert_count)
    page_count = group_rows // PAGE
    group = lax.axis_index("req")
    member = lax.axis_index(MEMBER)
    holds_request = (request_groups == group).astype(jnp.int32)
    my_lengths = jnp.sum(holds_request[:, None] * prompt_lengths, axis=0)
    my_pages = jnp.sum(holds_request[:, None] * page_table, axis=0)
    starts = jnp.cumsum(my_lengths) - my_lengths
    first_row = member * tok_rows
    my_segments = lax.dynamic_slice_in_dim(segment_ids, first_row, tok_rows, 0)
    prompt_index = jnp.arange(prompt_lengths.shape[1], dtype=jnp.int32)
    token_start = jnp.sum(
        jnp.where(my_segments[:, None] == prompt_index[None, :], starts[None, :], 0), axis=1
    )
    positions = (first_row + jnp.arange(tok_rows, dtype=jnp.int32) - token_start).astype(
        jnp.float32
    )
    query_turned = rotate(query_vectors, positions)
    key_turned = rotate(key_vectors, positions)
    head_chunks = jnp.stack([query_turned, key_turned, value_vectors]).reshape(
        3, tok_rows, member_count, model_width // member_count
    )
    qkv_group = lax.all_to_all(
        head_chunks.transpose(0, 2, 1, 3), MEMBER, split_axis=1, concat_axis=2, tiled=True
    )
    query_group, key_group, value_group = qkv_group[0, 0], qkv_group[1, 0], qkv_group[2, 0]
    column_count = key_group.shape[1]
    stacked = jnp.stack(
        [
            key_group.reshape(page_count, PAGE, column_count),
            value_group.reshape(page_count, PAGE, column_count),
        ],
        axis=1,
    ).reshape(page_count, -1)
    owner_of_page = my_pages // page_count
    group_range = jnp.arange(req_count, dtype=jnp.int32)
    shift_target = (group + group_range) % req_count
    send_select = (owner_of_page[None, :] == shift_target[:, None]).astype(jnp.bfloat16)
    outgoing_pages = (
        jnp.dot(send_select, stacked, preferred_element_type=jnp.float32)
        .astype(jnp.bfloat16)
        .reshape(req_count, 2, PAGE, column_count)
    )
    arriving = [outgoing_pages[0]]
    for shift in range(1, req_count):
        pairs = [(source, (source + shift) % req_count) for source in range(req_count)]
        arriving.append(lax.ppermute(outgoing_pages[shift], "req", pairs))
    incoming_pages = jnp.stack(arriving).reshape(req_count, -1)
    source_holds = (request_groups[None, :] == group_range[:, None]).astype(jnp.int32)
    source_pages = jnp.sum(source_holds[:, :, None] * page_table[None, :, :], axis=1)
    shift_source = (group - group_range + req_count) % req_count
    rolled_pages = jnp.sum(
        (shift_source[:, None] == group_range[None, :]).astype(jnp.int32)[:, :, None]
        * source_pages[None, :, :],
        axis=1,
    )
    slot_ids = group * page_count + jnp.arange(page_count, dtype=jnp.int32)
    place_select = jnp.sum(
        (rolled_pages[None, :, :] == slot_ids[:, None, None]).astype(jnp.int32), axis=2
    ).astype(jnp.bfloat16)
    kv_pages = (
        jnp.dot(place_select, incoming_pages, preferred_element_type=jnp.float32)
        .astype(jnp.bfloat16)
        .reshape(page_count, 2, PAGE, column_count)
    )
    heads_here = column_count // HEAD
    query_heads = query_group.reshape(group_rows, heads_here, HEAD)
    key_heads = key_group.reshape(group_rows, heads_here, HEAD)
    value_heads = value_group.reshape(group_rows, heads_here, HEAD)
    block_rows = group_rows
    attended = attend_all(query_heads, key_heads, value_heads, segment_ids, block_rows)
    token_heads = lax.all_to_all(attended, MEMBER, split_axis=0, concat_axis=1, tiled=True)
    hidden = residual.astype(jnp.float32) + jnp.dot(
        token_heads, out_weight, preferred_element_type=jnp.float32
    )
    normed = (
        hidden * lax.rsqrt(jnp.mean(hidden * hidden, axis=-1, keepdims=True) + norm_eps) * norm_gain
    ).astype(jnp.bfloat16)
    expert_range = jnp.arange(expert_count, dtype=jnp.int32)
    chosen = (expert_ids[:, :, None] == expert_range[None, None, :]).astype(jnp.int32)
    picked = jnp.sum(chosen, axis=1)
    earlier = jnp.cumsum(picked, axis=0) - picked
    slot_rank = jnp.sum(chosen * earlier[:, None, :], axis=2)
    slot_index = expert_ids * capacity + slot_rank
    slot_range = jnp.arange(expert_count * capacity, dtype=jnp.int32)
    dispatch_matrix = jnp.sum(
        (slot_index[None, :, :] == slot_range[:, None, None]).astype(jnp.int32), axis=2
    ).astype(jnp.bfloat16)
    combine = jnp.sum(
        jnp.where(slot_index[:, :, None] == slot_range[None, None, :], gate_weights[:, :, None], 0.0),
        axis=1,
    )
    combine_high = combine.astype(jnp.bfloat16)
    combine_low = (combine - combine_high.astype(jnp.float32)).astype(jnp.bfloat16)
    combine_parts = jnp.concatenate([combine_high, combine_low], axis=0).reshape(
        2 * tok_rows, expert_count, capacity
    )
    dispatch_slots = dispatch_matrix.reshape(expert_count, capacity, tok_rows)
    inner_both = jnp.concatenate([expert_inner[0], partner_inner[0]], axis=1)
    outer_both = jnp.concatenate([expert_outer[0], partner_outer[0]], axis=0)
    first_rows = 2 * capacity // 3
    arrived = []
    for low_slot, high_slot in ((0, first_rows), (first_rows, capacity)):
        chunk_rows = high_slot - low_slot
        chunk_select = dispatch_slots[:, low_slot:high_slot].reshape(expert_count * chunk_rows, tok_rows)
        packed = jnp.dot(chunk_select, normed, preferred_element_type=jnp.float32).astype(jnp.bfloat16)
        arrived.append(send_rows(packed.reshape(expert_count, chunk_rows, model_width)))
    mixed = jnp.zeros((tok_rows, model_width), jnp.float32)
    for (low_slot, high_slot), expert_input in zip(((0, first_rows), (first_rows, capacity)), arrived):
        chunk_rows = high_slot - low_slot
        expert_out = full_expert(
            expert_input.reshape(expert_count * chunk_rows, model_width), inner_both, outer_both
        )
        returned = send_back(expert_out.reshape(expert_count, chunk_rows, model_width)).reshape(
            expert_count * chunk_rows, model_width
        )
        parts = combine_parts[:, :, low_slot:high_slot].reshape(2 * tok_rows, expert_count * chunk_rows)
        both_parts = jnp.dot(parts, returned, preferred_element_type=jnp.float32)
        mixed = mixed + both_parts[:tok_rows] + both_parts[tok_rows:]
    layer_out = (hidden + mixed).astype(jnp.bfloat16)
    return (layer_out, kv_pages)


def solution(mesh):
    req_count, member_count = mesh.devices.shape
    fine = Mesh(mesh.devices.reshape(req_count, member_count // 2, 2), EVERY)
    token_rows = P(EVERY, None)
    placed = (
        token_rows,
        token_rows,
        token_rows,
        token_rows,
        P("req"),
        P(),
        P(),
        P(),
        token_rows,
        token_rows,
        P(),
        P(),
        P(EVERY, None, None),
        P(EVERY, None, None),
    )
    return jax.shard_map(
        on_device,
        mesh=fine,
        in_specs=placed,
        out_specs=(token_rows, P("req", None, None, MEMBER)),
        check_vma=False,
    )
```

```python
import jax
import jax.numpy as jnp
from jax import lax
from jax.sharding import Mesh, PartitionSpec as P

HEAD = 128
PAGE = 128
MEMBER = ("x", "core")
EXPERT_AXES = ("req", "x")
EVERY = ("req", "x", "core")


rope_base = 10000.0
norm_eps = 1e-06
masked_score = -1e30


def partner(value, axis, distance):
    return lax.ppermute(value, axis, [(i, i ^ 1 << distance) for i in range(lax.axis_size(axis))])


def rotate(values_in, positions):
    row_count = values_in.shape[0]
    half_head = HEAD // 2
    inverse = rope_base ** (-(2.0 * jnp.arange(half_head, dtype=jnp.float32)) / HEAD)
    angles = positions[:, None] * inverse[None, :]
    cosine = jnp.cos(angles)[:, None, :]
    sines = jnp.sin(angles)[:, None, :]
    shaped = values_in.astype(jnp.float32).reshape(row_count, -1, HEAD)
    first_half = shaped[..., :half_head]
    second_half = shaped[..., half_head:]
    turned = jnp.concatenate(
        [first_half * cosine - second_half * sines, second_half * cosine + first_half * sines],
        axis=-1,
    )
    return turned.reshape(row_count, -1).astype(jnp.bfloat16)


def score_block(query_block, query_segments, key_block, key_segments):
    scores = jnp.einsum(
        "qhd,khd->hqk", query_block, key_block, preferred_element_type=jnp.float32
    ) * HEAD ** (-0.5)
    same_prompt = (query_segments[:, None] == key_segments[None, :])[None]
    return (jnp.where(same_prompt, scores, masked_score), same_prompt)


def attend_all(query_heads, key_heads, value_heads, group_segments, block_rows):
    block_count = query_heads.shape[0] // block_rows

    def one_block(block_index):
        start_row = block_index * block_rows
        query_block = lax.dynamic_slice_in_dim(query_heads, start_row, block_rows, 0)
        query_segments = lax.dynamic_slice_in_dim(group_segments, start_row, block_rows, 0)
        scores, same_prompt = score_block(query_block, query_segments, key_heads, group_segments)
        top_score = jnp.max(scores, axis=-1, keepdims=True)
        weights = jnp.where(same_prompt, jnp.exp(scores - top_score), 0.0)
        totals = jnp.sum(weights, axis=-1)
        mixed = jnp.einsum(
            "hqk,khd->qhd",
            weights.astype(jnp.bfloat16),
            value_heads,
            preferred_element_type=jnp.float32,
        )
        return (mixed / totals.T[:, :, None]).astype(jnp.bfloat16)

    results = lax.map(one_block, jnp.arange(block_count))
    return results.reshape(query_heads.shape[0], -1)


def send_rows(blocks):
    arrived = lax.all_to_all(blocks, EXPERT_AXES, split_axis=0, concat_axis=0, tiled=True)
    return arrived


def send_back(blocks):
    arrived = lax.all_to_all(blocks, EXPERT_AXES, split_axis=0, concat_axis=0, tiled=True)
    return arrived


def full_expert(rows, inner_both, outer_both):
    projected = jnp.dot(rows, inner_both, preferred_element_type=jnp.float32)
    quarter = projected.shape[1] // 4
    active = jnp.concatenate(
        [
            jax.nn.silu(projected[:, :quarter]) * projected[:, quarter : 2 * quarter],
            jax.nn.silu(projected[:, 2 * quarter : 3 * quarter]) * projected[:, 3 * quarter :],
        ],
        axis=1,
    ).astype(jnp.bfloat16)
    return jnp.dot(active, outer_both, preferred_element_type=jnp.float32).astype(jnp.bfloat16)


def on_device(
    residual,
    query_vectors,
    key_vectors,
    value_vectors,
    segment_ids,
    prompt_lengths,
    request_groups,
    page_table,
    expert_ids,
    gate_weights,
    out_weight,
    norm_gain,
    expert_inner,
    expert_outer,
):
    partner_inner = partner(expert_inner, "core", 0)
    partner_outer = partner(expert_outer, "core", 0)
    tok_rows, model_width = residual.shape
    req_count = lax.axis_size("req")
    member_count = lax.axis_size("x") * lax.axis_size("core")
    device_count = req_count * member_count
    expert_count = device_count // 2
    group_rows = tok_rows * member_count
    top_count = expert_ids.shape[1]
    capacity = 3 * tok_rows * top_count // (2 * expert_count)
    page_count = group_rows // PAGE
    group = lax.axis_index("req")
    member = lax.axis_index(MEMBER)
    holds_request = (request_groups == group).astype(jnp.int32)
    my_lengths = jnp.sum(holds_request[:, None] * prompt_lengths, axis=0)
    my_pages = jnp.sum(holds_request[:, None] * page_table, axis=0)
    starts = jnp.cumsum(my_lengths) - my_lengths
    first_row = member * tok_rows
    my_segments = lax.dynamic_slice_in_dim(segment_ids, first_row, tok_rows, 0)
    prompt_index = jnp.arange(prompt_lengths.shape[1], dtype=jnp.int32)
    token_start = jnp.sum(
        jnp.where(my_segments[:, None] == prompt_index[None, :], starts[None, :], 0), axis=1
    )
    positions = (first_row + jnp.arange(tok_rows, dtype=jnp.int32) - token_start).astype(
        jnp.float32
    )
    query_turned = rotate(query_vectors, positions)
    key_turned = rotate(key_vectors, positions)
    head_chunks = jnp.stack([query_turned, key_turned, value_vectors]).reshape(
        3, tok_rows, member_count, model_width // member_count
    )
    qkv_group = lax.all_to_all(
        head_chunks.transpose(0, 2, 1, 3), MEMBER, split_axis=1, concat_axis=2, tiled=True
    )
    query_group, key_group, value_group = qkv_group[0, 0], qkv_group[1, 0], qkv_group[2, 0]
    column_count = key_group.shape[1]
    stacked = jnp.stack(
        [
            key_group.reshape(page_count, PAGE, column_count),
            value_group.reshape(page_count, PAGE, column_count),
        ],
        axis=1,
    ).reshape(page_count, -1)
    owner_of_page = my_pages // page_count
    group_range = jnp.arange(req_count, dtype=jnp.int32)
    page_range = jnp.arange(page_count, dtype=jnp.int32)
    page_blocks = stacked.reshape(page_count, 2, PAGE, column_count)
    arriving = []
    for shift in range(req_count):
        target = (group + shift) % req_count
        page_pick = jnp.max(jnp.where(owner_of_page == target, page_range, 0))
        page_out = lax.dynamic_index_in_dim(page_blocks, page_pick, 0, keepdims=False)
        if shift:
            pairs = [(source, (source + shift) % req_count) for source in range(req_count)]
            page_out = lax.ppermute(page_out, "req", pairs)
        arriving.append(page_out)
    source_holds = (request_groups[None, :] == group_range[:, None]).astype(jnp.int32)
    source_pages = jnp.sum(source_holds[:, :, None] * page_table[None, :, :], axis=1)
    shift_source = (group - group_range + req_count) % req_count
    rolled_pages = jnp.sum(
        (shift_source[:, None] == group_range[None, :]).astype(jnp.int32)[:, :, None]
        * source_pages[None, :, :],
        axis=1,
    )
    slot_ids = group * page_count + page_range
    slot_shift = jnp.sum(
        jnp.where(
            jnp.any(rolled_pages[None, :, :] == slot_ids[:, None, None], axis=2),
            group_range[None, :],
            0,
        ),
        axis=1,
    )
    heads_here = column_count // HEAD
    query_heads = query_group.reshape(group_rows, heads_here, HEAD)
    key_heads = key_group.reshape(group_rows, heads_here, HEAD)
    value_heads = value_group.reshape(group_rows, heads_here, HEAD)
    block_rows = group_rows
    attended = attend_all(query_heads, key_heads, value_heads, segment_ids, block_rows)
    token_heads = lax.all_to_all(attended, MEMBER, split_axis=0, concat_axis=1, tiled=True)
    hidden = residual.astype(jnp.float32) + jnp.dot(
        token_heads, out_weight, preferred_element_type=jnp.float32
    )
    normed = (
        hidden * lax.rsqrt(jnp.mean(hidden * hidden, axis=-1, keepdims=True) + norm_eps) * norm_gain
    ).astype(jnp.bfloat16)
    arriving, normed = lax.optimization_barrier((arriving, normed))
    kv_pages = jnp.stack(arriving)[slot_shift]
    expert_range = jnp.arange(expert_count, dtype=jnp.int32)
    chosen = (expert_ids[:, :, None] == expert_range[None, None, :]).astype(jnp.int32)
    picked = jnp.sum(chosen, axis=1)
    earlier = jnp.cumsum(picked, axis=0) - picked
    slot_rank = jnp.sum(chosen * earlier[:, None, :], axis=2)
    slot_index = expert_ids * capacity + slot_rank
    slot_range = jnp.arange(expert_count * capacity, dtype=jnp.int32)
    dispatch_matrix = jnp.sum(
        (slot_index[None, :, :] == slot_range[:, None, None]).astype(jnp.int32), axis=2
    ).astype(jnp.bfloat16)
    combine = jnp.sum(
        jnp.where(slot_index[:, :, None] == slot_range[None, None, :], gate_weights[:, :, None], 0.0),
        axis=1,
    )
    combine_high = combine.astype(jnp.bfloat16)
    combine_low = (combine - combine_high.astype(jnp.float32)).astype(jnp.bfloat16)
    combine_parts = jnp.concatenate([combine_high, combine_low], axis=0).reshape(
        2 * tok_rows, expert_count, capacity
    )
    dispatch_slots = dispatch_matrix.reshape(expert_count, capacity, tok_rows)
    inner_both = jnp.concatenate([expert_inner[0], partner_inner[0]], axis=1)
    outer_both = jnp.concatenate([expert_outer[0], partner_outer[0]], axis=0)
    first_rows = 2 * capacity // 3
    arrived = []
    for low_slot, high_slot in ((0, first_rows), (first_rows, capacity)):
        chunk_rows = high_slot - low_slot
        chunk_select = dispatch_slots[:, low_slot:high_slot].reshape(expert_count * chunk_rows, tok_rows)
        packed = jnp.dot(chunk_select, normed, preferred_element_type=jnp.float32).astype(jnp.bfloat16)
        arrived.append(send_rows(packed.reshape(expert_count, chunk_rows, model_width)))
    mixed = jnp.zeros((tok_rows, model_width), jnp.float32)
    for (low_slot, high_slot), expert_input in zip(((0, first_rows), (first_rows, capacity)), arrived):
        chunk_rows = high_slot - low_slot
        expert_out = full_expert(
            expert_input.reshape(expert_count * chunk_rows, model_width), inner_both, outer_both
        )
        returned = send_back(expert_out.reshape(expert_count, chunk_rows, model_width)).reshape(
            expert_count * chunk_rows, model_width
        )
        parts = combine_parts[:, :, low_slot:high_slot].reshape(2 * tok_rows, expert_count * chunk_rows)
        both_parts = jnp.dot(parts, returned, preferred_element_type=jnp.float32)
        mixed = mixed + both_parts[:tok_rows] + both_parts[tok_rows:]
    layer_out = (hidden + mixed).astype(jnp.bfloat16)
    return (layer_out, kv_pages)


def solution(mesh):
    req_count, member_count = mesh.devices.shape
    fine = Mesh(mesh.devices.reshape(req_count, member_count // 2, 2), EVERY)
    token_rows = P(EVERY, None)
    placed = (
        token_rows,
        token_rows,
        token_rows,
        token_rows,
        P("req"),
        P(),
        P(),
        P(),
        token_rows,
        token_rows,
        P(),
        P(),
        P(EVERY, None, None),
        P(EVERY, None, None),
    )
    return jax.shard_map(
        on_device,
        mesh=fine,
        in_specs=placed,
        out_specs=(token_rows, P("req", None, None, MEMBER)),
        check_vma=False,
    )
```

```python
import jax
import jax.numpy as jnp
from jax import lax
from jax.sharding import Mesh, PartitionSpec as P

HEAD = 128
PAGE = 128
MEMBER = ("x", "core")
EXPERT_AXES = ("req", "x")
EVERY = ("req", "x", "core")


rope_base = 10000.0
norm_eps = 1e-06
masked_score = -1e30


def partner(value, axis, distance):
    return lax.ppermute(value, axis, [(i, i ^ 1 << distance) for i in range(lax.axis_size(axis))])


def rotate(values_in, positions):
    row_count = values_in.shape[0]
    half_head = HEAD // 2
    inverse = rope_base ** (-(2.0 * jnp.arange(half_head, dtype=jnp.float32)) / HEAD)
    angles = positions[:, None] * inverse[None, :]
    cosine = jnp.cos(angles)[:, None, :]
    sines = jnp.sin(angles)[:, None, :]
    shaped = values_in.astype(jnp.float32).reshape(row_count, -1, HEAD)
    first_half = shaped[..., :half_head]
    second_half = shaped[..., half_head:]
    turned = jnp.concatenate(
        [first_half * cosine - second_half * sines, second_half * cosine + first_half * sines],
        axis=-1,
    )
    return turned.reshape(row_count, -1).astype(jnp.bfloat16)


def score_block(query_block, query_segments, key_block, key_segments):
    scores = jnp.einsum(
        "qhd,khd->hqk", query_block, key_block, preferred_element_type=jnp.float32
    ) * HEAD ** (-0.5)
    same_prompt = (query_segments[:, None] == key_segments[None, :])[None]
    return (jnp.where(same_prompt, scores, masked_score), same_prompt)


def attend_all(query_heads, key_heads, value_heads, group_segments, block_rows):
    block_count = query_heads.shape[0] // block_rows

    def one_block(block_index):
        start_row = block_index * block_rows
        query_block = lax.dynamic_slice_in_dim(query_heads, start_row, block_rows, 0)
        query_segments = lax.dynamic_slice_in_dim(group_segments, start_row, block_rows, 0)
        scores, same_prompt = score_block(query_block, query_segments, key_heads, group_segments)
        top_score = jnp.max(scores, axis=-1, keepdims=True)
        weights = jnp.where(same_prompt, jnp.exp(scores - top_score), 0.0)
        totals = jnp.sum(weights, axis=-1)
        mixed = jnp.einsum(
            "hqk,khd->qhd",
            weights.astype(jnp.bfloat16),
            value_heads,
            preferred_element_type=jnp.float32,
        )
        return (mixed / totals.T[:, :, None]).astype(jnp.bfloat16)

    results = lax.map(one_block, jnp.arange(block_count))
    return results.reshape(query_heads.shape[0], -1)


def send_rows(blocks):
    arrived = lax.all_to_all(blocks, EXPERT_AXES, split_axis=0, concat_axis=0, tiled=True)
    return arrived


def send_back(blocks):
    arrived = lax.all_to_all(blocks, EXPERT_AXES, split_axis=0, concat_axis=0, tiled=True)
    return arrived


def full_expert(rows, inner_both, outer_both):
    projected = jnp.dot(rows, inner_both, preferred_element_type=jnp.float32)
    quarter = projected.shape[1] // 4
    active = jnp.concatenate(
        [
            jax.nn.silu(projected[:, :quarter]) * projected[:, quarter : 2 * quarter],
            jax.nn.silu(projected[:, 2 * quarter : 3 * quarter]) * projected[:, 3 * quarter :],
        ],
        axis=1,
    ).astype(jnp.bfloat16)
    return jnp.dot(active, outer_both, preferred_element_type=jnp.float32).astype(jnp.bfloat16)


def on_device(
    residual,
    query_vectors,
    key_vectors,
    value_vectors,
    segment_ids,
    prompt_lengths,
    request_groups,
    page_table,
    expert_ids,
    gate_weights,
    out_weight,
    norm_gain,
    expert_inner,
    expert_outer,
):
    partner_inner = partner(expert_inner, "core", 0)
    partner_outer = partner(expert_outer, "core", 0)
    tok_rows, model_width = residual.shape
    req_count = lax.axis_size("req")
    member_count = lax.axis_size("x") * lax.axis_size("core")
    device_count = req_count * member_count
    expert_count = device_count // 2
    group_rows = tok_rows * member_count
    top_count = expert_ids.shape[1]
    capacity = 3 * tok_rows * top_count // (2 * expert_count)
    page_count = group_rows // PAGE
    group = lax.axis_index("req")
    member = lax.axis_index(MEMBER)
    holds_request = (request_groups == group).astype(jnp.int32)
    my_lengths = jnp.sum(holds_request[:, None] * prompt_lengths, axis=0)
    my_pages = jnp.sum(holds_request[:, None] * page_table, axis=0)
    starts = jnp.cumsum(my_lengths) - my_lengths
    first_row = member * tok_rows
    my_segments = lax.dynamic_slice_in_dim(segment_ids, first_row, tok_rows, 0)
    prompt_index = jnp.arange(prompt_lengths.shape[1], dtype=jnp.int32)
    token_start = jnp.sum(
        jnp.where(my_segments[:, None] == prompt_index[None, :], starts[None, :], 0), axis=1
    )
    positions = (first_row + jnp.arange(tok_rows, dtype=jnp.int32) - token_start).astype(
        jnp.float32
    )
    query_turned = rotate(query_vectors, positions)
    key_turned = rotate(key_vectors, positions)
    head_chunks = jnp.stack([query_turned, key_turned, value_vectors]).reshape(
        3, tok_rows, member_count, model_width // member_count
    )
    qkv_group = lax.all_to_all(
        head_chunks.transpose(0, 2, 1, 3), MEMBER, split_axis=1, concat_axis=2, tiled=True
    )
    query_group, key_group, value_group = qkv_group[0, 0], qkv_group[1, 0], qkv_group[2, 0]
    column_count = key_group.shape[1]
    stacked = jnp.stack(
        [
            key_group.reshape(page_count, PAGE, column_count),
            value_group.reshape(page_count, PAGE, column_count),
        ],
        axis=1,
    ).reshape(page_count, -1)
    owner_of_page = my_pages // page_count
    group_range = jnp.arange(req_count, dtype=jnp.int32)
    send_select = (owner_of_page[None, :] == group_range[:, None]).astype(jnp.bfloat16)
    outgoing_pages = jnp.dot(send_select, stacked, preferred_element_type=jnp.float32).astype(
        jnp.bfloat16
    )
    incoming_pages = lax.all_to_all(outgoing_pages, "req", split_axis=0, concat_axis=0, tiled=True)
    source_holds = (request_groups[None, :] == group_range[:, None]).astype(jnp.int32)
    source_pages = jnp.sum(source_holds[:, :, None] * page_table[None, :, :], axis=1)
    slot_ids = group * page_count + jnp.arange(page_count, dtype=jnp.int32)
    place_select = jnp.sum(
        (source_pages[None, :, :] == slot_ids[:, None, None]).astype(jnp.int32), axis=2
    ).astype(jnp.bfloat16)
    kv_pages = (
        jnp.dot(place_select, incoming_pages, preferred_element_type=jnp.float32)
        .astype(jnp.bfloat16)
        .reshape(page_count, 2, PAGE, column_count)
    )
    heads_here = column_count // HEAD
    query_heads = query_group.reshape(group_rows, heads_here, HEAD)
    key_heads = key_group.reshape(group_rows, heads_here, HEAD)
    value_heads = value_group.reshape(group_rows, heads_here, HEAD)
    block_rows = group_rows
    attended = attend_all(query_heads, key_heads, value_heads, segment_ids, block_rows)
    token_heads = lax.all_to_all(attended, MEMBER, split_axis=0, concat_axis=1, tiled=True)
    hidden = residual.astype(jnp.float32) + jnp.dot(
        token_heads, out_weight, preferred_element_type=jnp.float32
    )
    normed = (
        hidden * lax.rsqrt(jnp.mean(hidden * hidden, axis=-1, keepdims=True) + norm_eps) * norm_gain
    ).astype(jnp.bfloat16)
    partner_inner, partner_outer, normed = lax.optimization_barrier((partner_inner, partner_outer, normed))
    expert_range = jnp.arange(expert_count, dtype=jnp.int32)
    chosen = (expert_ids[:, :, None] == expert_range[None, None, :]).astype(jnp.int32)
    picked = jnp.sum(chosen, axis=1)
    earlier = jnp.cumsum(picked, axis=0) - picked
    slot_rank = jnp.sum(chosen * earlier[:, None, :], axis=2)
    slot_index = expert_ids * capacity + slot_rank
    slot_range = jnp.arange(expert_count * capacity, dtype=jnp.int32)
    dispatch_matrix = jnp.sum(
        (slot_index[None, :, :] == slot_range[:, None, None]).astype(jnp.int32), axis=2
    ).astype(jnp.bfloat16)
    packed = (
        jnp.dot(dispatch_matrix, normed, preferred_element_type=jnp.float32)
        .astype(jnp.bfloat16)
        .reshape(expert_count, capacity, model_width)
    )
    expert_input = send_rows(packed)
    flat_input = expert_input.reshape(expert_count * capacity, model_width)
    inner_both = jnp.concatenate([expert_inner[0], partner_inner[0]], axis=1)
    outer_both = jnp.concatenate([expert_outer[0], partner_outer[0]], axis=0)
    expert_out = full_expert(flat_input, inner_both, outer_both).reshape(
        expert_count, capacity, model_width
    )
    returned = send_back(expert_out).reshape(expert_count * capacity, model_width)
    combine = jnp.sum(
        jnp.where(slot_index[:, :, None] == slot_range[None, None, :], gate_weights[:, :, None], 0.0),
        axis=1,
    )
    combine_high = combine.astype(jnp.bfloat16)
    combine_low = (combine - combine_high.astype(jnp.float32)).astype(jnp.bfloat16)
    both_parts = jnp.dot(
        jnp.concatenate([combine_high, combine_low], axis=0), returned, preferred_element_type=jnp.float32
    )
    mixed = both_parts[:tok_rows] + both_parts[tok_rows:]
    layer_out = (hidden + mixed).astype(jnp.bfloat16)
    return (layer_out, kv_pages)


def solution(mesh):
    req_count, member_count = mesh.devices.shape
    fine = Mesh(mesh.devices.reshape(req_count, member_count // 2, 2), EVERY)
    token_rows = P(EVERY, None)
    placed = (
        token_rows,
        token_rows,
        token_rows,
        token_rows,
        P("req"),
        P(),
        P(),
        P(),
        token_rows,
        token_rows,
        P(),
        P(),
        P(EVERY, None, None),
        P(EVERY, None, None),
    )
    return jax.shard_map(
        on_device,
        mesh=fine,
        in_specs=placed,
        out_specs=(token_rows, P("req", None, None, MEMBER)),
        check_vma=False,
    )
```

```python
import jax
import jax.numpy as jnp
from jax import lax
from jax.sharding import Mesh, PartitionSpec as P

HEAD = 128
PAGE = 128
MEMBER = ("x", "core")
EXPERT_AXES = ("req", "x")
EVERY = ("req", "x", "core")


rope_base = 10000.0
norm_eps = 1e-06
masked_score = -1e30


def partner(value, axis, distance):
    return lax.ppermute(value, axis, [(i, i ^ 1 << distance) for i in range(lax.axis_size(axis))])


def rotate(values_in, positions):
    row_count = values_in.shape[0]
    half_head = HEAD // 2
    inverse = rope_base ** (-(2.0 * jnp.arange(half_head, dtype=jnp.float32)) / HEAD)
    angles = positions[:, None] * inverse[None, :]
    cosine = jnp.cos(angles)[:, None, :]
    sines = jnp.sin(angles)[:, None, :]
    shaped = values_in.astype(jnp.float32).reshape(row_count, -1, HEAD)
    first_half = shaped[..., :half_head]
    second_half = shaped[..., half_head:]
    turned = jnp.concatenate(
        [first_half * cosine - second_half * sines, second_half * cosine + first_half * sines],
        axis=-1,
    )
    return turned.reshape(row_count, -1).astype(jnp.bfloat16)


def score_block(query_block, query_segments, key_block, key_segments):
    scores = jnp.einsum(
        "qhd,khd->hqk", query_block, key_block, preferred_element_type=jnp.float32
    ) * HEAD ** (-0.5)
    same_prompt = (query_segments[:, None] == key_segments[None, :])[None]
    return (jnp.where(same_prompt, scores, masked_score), same_prompt)


def attend_all(query_heads, key_heads, value_heads, group_segments, block_rows):
    block_count = query_heads.shape[0] // block_rows

    def one_block(block_index):
        start_row = block_index * block_rows
        query_block = lax.dynamic_slice_in_dim(query_heads, start_row, block_rows, 0)
        query_segments = lax.dynamic_slice_in_dim(group_segments, start_row, block_rows, 0)
        scores, same_prompt = score_block(query_block, query_segments, key_heads, group_segments)
        top_score = jnp.max(scores, axis=-1, keepdims=True)
        weights = jnp.where(same_prompt, jnp.exp(scores - top_score), 0.0)
        totals = jnp.sum(weights, axis=-1)
        mixed = jnp.einsum(
            "hqk,khd->qhd",
            weights.astype(jnp.bfloat16),
            value_heads,
            preferred_element_type=jnp.float32,
        )
        return (mixed / totals.T[:, :, None]).astype(jnp.bfloat16)

    results = lax.map(one_block, jnp.arange(block_count))
    return results.reshape(query_heads.shape[0], -1)


def send_rows(blocks):
    arrived = lax.all_to_all(blocks, EXPERT_AXES, split_axis=0, concat_axis=0, tiled=True)
    return arrived


def send_back(blocks):
    arrived = lax.all_to_all(blocks, EXPERT_AXES, split_axis=0, concat_axis=0, tiled=True)
    return arrived


def full_expert(rows, inner_both, outer_both):
    projected = jnp.dot(rows, inner_both, preferred_element_type=jnp.float32)
    quarter = projected.shape[1] // 4
    active = jnp.concatenate(
        [
            jax.nn.silu(projected[:, :quarter]) * projected[:, quarter : 2 * quarter],
            jax.nn.silu(projected[:, 2 * quarter : 3 * quarter]) * projected[:, 3 * quarter :],
        ],
        axis=1,
    ).astype(jnp.bfloat16)
    return jnp.dot(active, outer_both, preferred_element_type=jnp.float32).astype(jnp.bfloat16)


def on_device(
    residual,
    query_vectors,
    key_vectors,
    value_vectors,
    segment_ids,
    prompt_lengths,
    request_groups,
    page_table,
    expert_ids,
    gate_weights,
    out_weight,
    norm_gain,
    expert_inner,
    expert_outer,
):
    partner_inner = partner(expert_inner, "core", 0)
    partner_outer = partner(expert_outer, "core", 0)
    tok_rows, model_width = residual.shape
    req_count = lax.axis_size("req")
    member_count = lax.axis_size("x") * lax.axis_size("core")
    device_count = req_count * member_count
    expert_count = device_count // 2
    group_rows = tok_rows * member_count
    top_count = expert_ids.shape[1]
    capacity = 3 * tok_rows * top_count // (2 * expert_count)
    page_count = group_rows // PAGE
    group = lax.axis_index("req")
    member = lax.axis_index(MEMBER)
    holds_request = (request_groups == group).astype(jnp.int32)
    my_lengths = jnp.sum(holds_request[:, None] * prompt_lengths, axis=0)
    my_pages = jnp.sum(holds_request[:, None] * page_table, axis=0)
    starts = jnp.cumsum(my_lengths) - my_lengths
    first_row = member * tok_rows
    my_segments = lax.dynamic_slice_in_dim(segment_ids, first_row, tok_rows, 0)
    prompt_index = jnp.arange(prompt_lengths.shape[1], dtype=jnp.int32)
    token_start = jnp.sum(
        jnp.where(my_segments[:, None] == prompt_index[None, :], starts[None, :], 0), axis=1
    )
    positions = (first_row + jnp.arange(tok_rows, dtype=jnp.int32) - token_start).astype(
        jnp.float32
    )
    query_turned = rotate(query_vectors, positions)
    key_turned = rotate(key_vectors, positions)
    head_chunks = jnp.stack([query_turned, key_turned, value_vectors]).reshape(
        3, tok_rows, member_count, model_width // member_count
    )
    qkv_group = lax.all_to_all(
        head_chunks.transpose(0, 2, 1, 3), MEMBER, split_axis=1, concat_axis=2, tiled=True
    )
    query_group, key_group, value_group = qkv_group[0, 0], qkv_group[1, 0], qkv_group[2, 0]
    column_count = key_group.shape[1]
    stacked = jnp.stack(
        [
            key_group.reshape(page_count, PAGE, column_count),
            value_group.reshape(page_count, PAGE, column_count),
        ],
        axis=1,
    ).reshape(page_count, -1)
    owner_of_page = my_pages // page_count
    group_range = jnp.arange(req_count, dtype=jnp.int32)
    send_select = (owner_of_page[None, :] == group_range[:, None]).astype(jnp.bfloat16)
    outgoing_pages = jnp.dot(send_select, stacked, preferred_element_type=jnp.float32).astype(
        jnp.bfloat16
    )
    incoming_pages = lax.all_to_all(outgoing_pages, "req", split_axis=0, concat_axis=0, tiled=True)
    source_holds = (request_groups[None, :] == group_range[:, None]).astype(jnp.int32)
    source_pages = jnp.sum(source_holds[:, :, None] * page_table[None, :, :], axis=1)
    slot_ids = group * page_count + jnp.arange(page_count, dtype=jnp.int32)
    place_select = jnp.sum(
        (source_pages[None, :, :] == slot_ids[:, None, None]).astype(jnp.int32), axis=2
    ).astype(jnp.bfloat16)
    heads_here = column_count // HEAD
    query_heads = query_group.reshape(group_rows, heads_here, HEAD)
    key_heads = key_group.reshape(group_rows, heads_here, HEAD)
    value_heads = value_group.reshape(group_rows, heads_here, HEAD)
    block_rows = group_rows
    attended = attend_all(query_heads, key_heads, value_heads, segment_ids, block_rows)
    incoming_pages, attended = lax.optimization_barrier((incoming_pages, attended))
    kv_pages = (
        jnp.dot(place_select, incoming_pages, preferred_element_type=jnp.float32)
        .astype(jnp.bfloat16)
        .reshape(page_count, 2, PAGE, column_count)
    )
    token_heads = lax.all_to_all(attended, MEMBER, split_axis=0, concat_axis=1, tiled=True)
    hidden = residual.astype(jnp.float32) + jnp.dot(
        token_heads, out_weight, preferred_element_type=jnp.float32
    )
    normed = (
        hidden * lax.rsqrt(jnp.mean(hidden * hidden, axis=-1, keepdims=True) + norm_eps) * norm_gain
    ).astype(jnp.bfloat16)
    partner_inner, partner_outer, normed = lax.optimization_barrier((partner_inner, partner_outer, normed))
    expert_range = jnp.arange(expert_count, dtype=jnp.int32)
    chosen = (expert_ids[:, :, None] == expert_range[None, None, :]).astype(jnp.int32)
    picked = jnp.sum(chosen, axis=1)
    earlier = jnp.cumsum(picked, axis=0) - picked
    slot_rank = jnp.sum(chosen * earlier[:, None, :], axis=2)
    slot_index = expert_ids * capacity + slot_rank
    slot_range = jnp.arange(expert_count * capacity, dtype=jnp.int32)
    dispatch_matrix = jnp.sum(
        (slot_index[None, :, :] == slot_range[:, None, None]).astype(jnp.int32), axis=2
    ).astype(jnp.bfloat16)
    combine = jnp.sum(
        jnp.where(slot_index[:, :, None] == slot_range[None, None, :], gate_weights[:, :, None], 0.0),
        axis=1,
    )
    combine_high = combine.astype(jnp.bfloat16)
    combine_low = (combine - combine_high.astype(jnp.float32)).astype(jnp.bfloat16)
    combine_parts = jnp.concatenate([combine_high, combine_low], axis=0).reshape(
        2 * tok_rows, expert_count, capacity
    )
    dispatch_slots = dispatch_matrix.reshape(expert_count, capacity, tok_rows)
    inner_both = jnp.concatenate([expert_inner[0], partner_inner[0]], axis=1)
    outer_both = jnp.concatenate([expert_outer[0], partner_outer[0]], axis=0)
    first_rows = 2 * capacity // 3
    chunk_bounds = ((0, first_rows), (first_rows, capacity))
    arrived = []
    for low_slot, high_slot in chunk_bounds:
        chunk_rows = high_slot - low_slot
        chunk_select = dispatch_slots[:, low_slot:high_slot].reshape(expert_count * chunk_rows, tok_rows)
        packed = jnp.dot(chunk_select, normed, preferred_element_type=jnp.float32).astype(jnp.bfloat16)
        arrived.append(send_rows(packed.reshape(expert_count, chunk_rows, model_width)))
    mixed = jnp.zeros((tok_rows, model_width), jnp.float32)
    for (low_slot, high_slot), expert_input in zip(chunk_bounds, arrived):
        chunk_rows = high_slot - low_slot
        expert_out = full_expert(
            expert_input.reshape(expert_count * chunk_rows, model_width), inner_both, outer_both
        )
        returned = send_back(expert_out.reshape(expert_count, chunk_rows, model_width)).reshape(
            expert_count * chunk_rows, model_width
        )
        parts = combine_parts[:, :, low_slot:high_slot].reshape(2 * tok_rows, expert_count * chunk_rows)
        both_parts = jnp.dot(parts, returned, preferred_element_type=jnp.float32)
        mixed = mixed + both_parts[:tok_rows] + both_parts[tok_rows:]
    layer_out = (hidden + mixed).astype(jnp.bfloat16)
    return (layer_out, kv_pages)


def solution(mesh):
    req_count, member_count = mesh.devices.shape
    fine = Mesh(mesh.devices.reshape(req_count, member_count // 2, 2), EVERY)
    token_rows = P(EVERY, None)
    placed = (
        token_rows,
        token_rows,
        token_rows,
        token_rows,
        P("req"),
        P(),
        P(),
        P(),
        token_rows,
        token_rows,
        P(),
        P(),
        P(EVERY, None, None),
        P(EVERY, None, None),
    )
    return jax.shard_map(
        on_device,
        mesh=fine,
        in_specs=placed,
        out_specs=(token_rows, P("req", None, None, MEMBER)),
        check_vma=False,
    )
```

```python
import jax
import jax.numpy as jnp
from jax import lax
from jax.sharding import Mesh, PartitionSpec as P

HEAD = 128
PAGE = 128
MEMBER = ("x", "core")
EXPERT_AXES = ("req", "x")
EVERY = ("req", "x", "core")


rope_base = 10000.0
norm_eps = 1e-06
masked_score = -1e30


def partner(value, axis, distance):
    return lax.ppermute(value, axis, [(i, i ^ 1 << distance) for i in range(lax.axis_size(axis))])


def rotate(values_in, positions):
    row_count = values_in.shape[0]
    half_head = HEAD // 2
    inverse = rope_base ** (-(2.0 * jnp.arange(half_head, dtype=jnp.float32)) / HEAD)
    angles = positions[:, None] * inverse[None, :]
    cosine = jnp.cos(angles)[:, None, :]
    sines = jnp.sin(angles)[:, None, :]
    shaped = values_in.astype(jnp.float32).reshape(row_count, -1, HEAD)
    first_half = shaped[..., :half_head]
    second_half = shaped[..., half_head:]
    turned = jnp.concatenate(
        [first_half * cosine - second_half * sines, second_half * cosine + first_half * sines],
        axis=-1,
    )
    return turned.reshape(row_count, -1).astype(jnp.bfloat16)


def score_block(query_block, query_segments, key_block, key_segments):
    scores = jnp.einsum(
        "qhd,khd->hqk", query_block, key_block, preferred_element_type=jnp.float32
    ) * HEAD ** (-0.5)
    same_prompt = (query_segments[:, None] == key_segments[None, :])[None]
    return (jnp.where(same_prompt, scores, masked_score), same_prompt)


def attend_all(query_heads, key_heads, value_heads, group_segments, block_rows):
    block_count = query_heads.shape[0] // block_rows

    def one_block(block_index):
        start_row = block_index * block_rows
        query_block = lax.dynamic_slice_in_dim(query_heads, start_row, block_rows, 0)
        query_segments = lax.dynamic_slice_in_dim(group_segments, start_row, block_rows, 0)
        scores, same_prompt = score_block(query_block, query_segments, key_heads, group_segments)
        top_score = jnp.max(scores, axis=-1, keepdims=True)
        weights = jnp.where(same_prompt, jnp.exp(scores - top_score), 0.0)
        totals = jnp.sum(weights, axis=-1)
        mixed = jnp.einsum(
            "hqk,khd->qhd",
            weights.astype(jnp.bfloat16),
            value_heads,
            preferred_element_type=jnp.float32,
        )
        return (mixed / totals.T[:, :, None]).astype(jnp.bfloat16)

    results = lax.map(one_block, jnp.arange(block_count))
    return results.reshape(query_heads.shape[0], -1)


def send_rows(blocks):
    arrived = lax.all_to_all(blocks, EXPERT_AXES, split_axis=0, concat_axis=0, tiled=True)
    return arrived


def send_back(blocks):
    arrived = lax.all_to_all(blocks, EXPERT_AXES, split_axis=0, concat_axis=0, tiled=True)
    return arrived


def full_expert(rows, inner_both, outer_both):
    projected = jnp.dot(rows, inner_both, preferred_element_type=jnp.float32)
    quarter = projected.shape[1] // 4
    active = jnp.concatenate(
        [
            jax.nn.silu(projected[:, :quarter]) * projected[:, quarter : 2 * quarter],
            jax.nn.silu(projected[:, 2 * quarter : 3 * quarter]) * projected[:, 3 * quarter :],
        ],
        axis=1,
    ).astype(jnp.bfloat16)
    return jnp.dot(active, outer_both, preferred_element_type=jnp.float32).astype(jnp.bfloat16)


def on_device(
    residual,
    query_vectors,
    key_vectors,
    value_vectors,
    segment_ids,
    prompt_lengths,
    request_groups,
    page_table,
    expert_ids,
    gate_weights,
    out_weight,
    norm_gain,
    expert_inner,
    expert_outer,
):
    partner_inner = partner(expert_inner, "core", 0)
    partner_outer = partner(expert_outer, "core", 0)
    tok_rows, model_width = residual.shape
    req_count = lax.axis_size("req")
    member_count = lax.axis_size("x") * lax.axis_size("core")
    device_count = req_count * member_count
    expert_count = device_count // 2
    group_rows = tok_rows * member_count
    top_count = expert_ids.shape[1]
    capacity = 3 * tok_rows * top_count // (2 * expert_count)
    page_count = group_rows // PAGE
    group = lax.axis_index("req")
    member = lax.axis_index(MEMBER)
    holds_request = (request_groups == group).astype(jnp.int32)
    my_lengths = jnp.sum(holds_request[:, None] * prompt_lengths, axis=0)
    my_pages = jnp.sum(holds_request[:, None] * page_table, axis=0)
    starts = jnp.cumsum(my_lengths) - my_lengths
    first_row = member * tok_rows
    my_segments = lax.dynamic_slice_in_dim(segment_ids, first_row, tok_rows, 0)
    prompt_index = jnp.arange(prompt_lengths.shape[1], dtype=jnp.int32)
    token_start = jnp.sum(
        jnp.where(my_segments[:, None] == prompt_index[None, :], starts[None, :], 0), axis=1
    )
    positions = (first_row + jnp.arange(tok_rows, dtype=jnp.int32) - token_start).astype(
        jnp.float32
    )
    query_turned = rotate(query_vectors, positions)
    key_turned = rotate(key_vectors, positions)
    head_chunks = jnp.stack([query_turned, key_turned, value_vectors]).reshape(
        3, tok_rows, member_count, model_width // member_count
    )
    qkv_group = lax.all_to_all(
        head_chunks.transpose(0, 2, 1, 3), MEMBER, split_axis=1, concat_axis=2, tiled=True
    )
    query_group, key_group, value_group = qkv_group[0, 0], qkv_group[1, 0], qkv_group[2, 0]
    column_count = key_group.shape[1]
    stacked = jnp.stack(
        [
            key_group.reshape(page_count, PAGE, column_count),
            value_group.reshape(page_count, PAGE, column_count),
        ],
        axis=1,
    ).reshape(page_count, -1)
    owner_of_page = my_pages // page_count
    group_range = jnp.arange(req_count, dtype=jnp.int32)
    page_range = jnp.arange(page_count, dtype=jnp.int32)
    page_blocks = stacked.reshape(page_count, 2, PAGE, column_count)
    sends_to = owner_of_page[None, :] == group_range[:, None]
    page_for_group = jnp.sum(jnp.where(sends_to, page_range[None, :], 0), axis=1)
    outgoing_pages = jnp.where(
        jnp.any(sends_to, axis=1)[:, None, None, None], page_blocks[page_for_group], jnp.zeros_like(page_blocks[:1])
    )
    incoming_pages = lax.all_to_all(outgoing_pages, "req", split_axis=0, concat_axis=0, tiled=True)
    source_holds = (request_groups[None, :] == group_range[:, None]).astype(jnp.int32)
    source_pages = jnp.sum(source_holds[:, :, None] * page_table[None, :, :], axis=1)
    slot_ids = group * page_count + page_range
    slot_source = jnp.sum(
        jnp.where(
            jnp.any(source_pages[None, :, :] == slot_ids[:, None, None], axis=2), group_range[None, :], 0
        ),
        axis=1,
    )
    heads_here = column_count // HEAD
    query_heads = query_group.reshape(group_rows, heads_here, HEAD)
    key_heads = key_group.reshape(group_rows, heads_here, HEAD)
    value_heads = value_group.reshape(group_rows, heads_here, HEAD)
    block_rows = group_rows
    attended = attend_all(query_heads, key_heads, value_heads, segment_ids, block_rows)
    incoming_pages, attended = lax.optimization_barrier((incoming_pages, attended))
    kv_pages = incoming_pages[slot_source]
    token_heads = lax.all_to_all(attended, MEMBER, split_axis=0, concat_axis=1, tiled=True)
    hidden = residual.astype(jnp.float32) + jnp.dot(
        token_heads, out_weight, preferred_element_type=jnp.float32
    )
    normed = (
        hidden * lax.rsqrt(jnp.mean(hidden * hidden, axis=-1, keepdims=True) + norm_eps) * norm_gain
    ).astype(jnp.bfloat16)
    partner_inner, partner_outer, normed = lax.optimization_barrier((partner_inner, partner_outer, normed))
    expert_range = jnp.arange(expert_count, dtype=jnp.int32)
    chosen = (expert_ids[:, :, None] == expert_range[None, None, :]).astype(jnp.int32)
    picked = jnp.sum(chosen, axis=1)
    earlier = jnp.cumsum(picked, axis=0) - picked
    slot_rank = jnp.sum(chosen * earlier[:, None, :], axis=2)
    slot_index = expert_ids * capacity + slot_rank
    slot_range = jnp.arange(expert_count * capacity, dtype=jnp.int32)
    dispatch_matrix = jnp.sum(
        (slot_index[None, :, :] == slot_range[:, None, None]).astype(jnp.int32), axis=2
    ).astype(jnp.bfloat16)
    combine = jnp.sum(
        jnp.where(slot_index[:, :, None] == slot_range[None, None, :], gate_weights[:, :, None], 0.0),
        axis=1,
    )
    combine_high = combine.astype(jnp.bfloat16)
    combine_low = (combine - combine_high.astype(jnp.float32)).astype(jnp.bfloat16)
    combine_parts = jnp.concatenate([combine_high, combine_low], axis=0).reshape(
        2 * tok_rows, expert_count, capacity
    )
    dispatch_slots = dispatch_matrix.reshape(expert_count, capacity, tok_rows)
    inner_both = jnp.concatenate([expert_inner[0], partner_inner[0]], axis=1)
    outer_both = jnp.concatenate([expert_outer[0], partner_outer[0]], axis=0)
    first_rows = 2 * capacity // 3
    chunk_bounds = ((0, first_rows), (first_rows, capacity))
    arrived = []
    for low_slot, high_slot in chunk_bounds:
        chunk_rows = high_slot - low_slot
        chunk_select = dispatch_slots[:, low_slot:high_slot].reshape(expert_count * chunk_rows, tok_rows)
        packed = jnp.dot(chunk_select, normed, preferred_element_type=jnp.float32).astype(jnp.bfloat16)
        arrived.append(send_rows(packed.reshape(expert_count, chunk_rows, model_width)))
    mixed = jnp.zeros((tok_rows, model_width), jnp.float32)
    for (low_slot, high_slot), expert_input in zip(chunk_bounds, arrived):
        chunk_rows = high_slot - low_slot
        expert_out = full_expert(
            expert_input.reshape(expert_count * chunk_rows, model_width), inner_both, outer_both
        )
        returned = send_back(expert_out.reshape(expert_count, chunk_rows, model_width)).reshape(
            expert_count * chunk_rows, model_width
        )
        parts = combine_parts[:, :, low_slot:high_slot].reshape(2 * tok_rows, expert_count * chunk_rows)
        both_parts = jnp.dot(parts, returned, preferred_element_type=jnp.float32)
        mixed = mixed + both_parts[:tok_rows] + both_parts[tok_rows:]
    layer_out = (hidden + mixed).astype(jnp.bfloat16)
    return (layer_out, kv_pages)


def solution(mesh):
    req_count, member_count = mesh.devices.shape
    fine = Mesh(mesh.devices.reshape(req_count, member_count // 2, 2), EVERY)
    token_rows = P(EVERY, None)
    placed = (
        token_rows,
        token_rows,
        token_rows,
        token_rows,
        P("req"),
        P(),
        P(),
        P(),
        token_rows,
        token_rows,
        P(),
        P(),
        P(EVERY, None, None),
        P(EVERY, None, None),
    )
    return jax.shard_map(
        on_device,
        mesh=fine,
        in_specs=placed,
        out_specs=(token_rows, P("req", None, None, MEMBER)),
        check_vma=False,
    )
```

```python
import jax
import jax.numpy as jnp
from jax import lax
from jax.sharding import Mesh, PartitionSpec as P

HEAD = 128
PAGE = 128
MEMBER = ("x", "core")
EXPERT_AXES = ("req", "x")
EVERY = ("req", "x", "core")


rope_base = 10000.0
norm_eps = 1e-06
masked_score = -1e30


def partner(value, axis, distance):
    return lax.ppermute(value, axis, [(i, i ^ 1 << distance) for i in range(lax.axis_size(axis))])


def rotate(values_in, positions):
    row_count = values_in.shape[0]
    half_head = HEAD // 2
    inverse = rope_base ** (-(2.0 * jnp.arange(half_head, dtype=jnp.float32)) / HEAD)
    angles = positions[:, None] * inverse[None, :]
    cosine = jnp.cos(angles)[:, None, :]
    sines = jnp.sin(angles)[:, None, :]
    shaped = values_in.astype(jnp.float32).reshape(row_count, -1, HEAD)
    first_half = shaped[..., :half_head]
    second_half = shaped[..., half_head:]
    turned = jnp.concatenate(
        [first_half * cosine - second_half * sines, second_half * cosine + first_half * sines],
        axis=-1,
    )
    return turned.reshape(row_count, -1).astype(jnp.bfloat16)


def score_block(query_block, query_segments, key_block, key_segments):
    scores = jnp.einsum(
        "qhd,khd->hqk", query_block, key_block, preferred_element_type=jnp.float32
    ) * HEAD ** (-0.5)
    same_prompt = (query_segments[:, None] == key_segments[None, :])[None]
    return (jnp.where(same_prompt, scores, masked_score), same_prompt)


def attend_all(query_heads, key_heads, value_heads, group_segments, block_rows):
    block_count = query_heads.shape[0] // block_rows

    def one_block(block_index):
        start_row = block_index * block_rows
        query_block = lax.dynamic_slice_in_dim(query_heads, start_row, block_rows, 0)
        query_segments = lax.dynamic_slice_in_dim(group_segments, start_row, block_rows, 0)
        scores, same_prompt = score_block(query_block, query_segments, key_heads, group_segments)
        top_score = jnp.max(scores, axis=-1, keepdims=True)
        weights = jnp.where(same_prompt, jnp.exp(scores - top_score), 0.0)
        totals = jnp.sum(weights, axis=-1)
        mixed = jnp.einsum(
            "hqk,khd->qhd",
            weights.astype(jnp.bfloat16),
            value_heads,
            preferred_element_type=jnp.float32,
        )
        return (mixed / totals.T[:, :, None]).astype(jnp.bfloat16)

    results = lax.map(one_block, jnp.arange(block_count))
    return results.reshape(query_heads.shape[0], -1)


def send_rows(blocks):
    arrived = lax.all_to_all(blocks, EXPERT_AXES, split_axis=0, concat_axis=0, tiled=True)
    return arrived


def send_back(blocks):
    arrived = lax.all_to_all(blocks, EXPERT_AXES, split_axis=0, concat_axis=0, tiled=True)
    return arrived


def full_expert(rows, inner_both, outer_both):
    projected = jnp.dot(rows, inner_both, preferred_element_type=jnp.float32)
    quarter = projected.shape[1] // 4
    active = jnp.concatenate(
        [
            jax.nn.silu(projected[:, :quarter]) * projected[:, quarter : 2 * quarter],
            jax.nn.silu(projected[:, 2 * quarter : 3 * quarter]) * projected[:, 3 * quarter :],
        ],
        axis=1,
    ).astype(jnp.bfloat16)
    return jnp.dot(active, outer_both, preferred_element_type=jnp.float32).astype(jnp.bfloat16)


def on_device(
    residual,
    query_vectors,
    key_vectors,
    value_vectors,
    segment_ids,
    prompt_lengths,
    request_groups,
    page_table,
    expert_ids,
    gate_weights,
    out_weight,
    norm_gain,
    expert_inner,
    expert_outer,
):
    partner_inner = partner(expert_inner, "core", 0)
    partner_outer = partner(expert_outer, "core", 0)
    tok_rows, model_width = residual.shape
    req_count = lax.axis_size("req")
    member_count = lax.axis_size("x") * lax.axis_size("core")
    device_count = req_count * member_count
    expert_count = device_count // 2
    group_rows = tok_rows * member_count
    top_count = expert_ids.shape[1]
    capacity = 3 * tok_rows * top_count // (2 * expert_count)
    page_count = group_rows // PAGE
    group = lax.axis_index("req")
    member = lax.axis_index(MEMBER)
    holds_request = (request_groups == group).astype(jnp.int32)
    my_lengths = jnp.sum(holds_request[:, None] * prompt_lengths, axis=0)
    my_pages = jnp.sum(holds_request[:, None] * page_table, axis=0)
    starts = jnp.cumsum(my_lengths) - my_lengths
    first_row = member * tok_rows
    my_segments = lax.dynamic_slice_in_dim(segment_ids, first_row, tok_rows, 0)
    prompt_index = jnp.arange(prompt_lengths.shape[1], dtype=jnp.int32)
    token_start = jnp.sum(
        jnp.where(my_segments[:, None] == prompt_index[None, :], starts[None, :], 0), axis=1
    )
    positions = (first_row + jnp.arange(tok_rows, dtype=jnp.int32) - token_start).astype(
        jnp.float32
    )
    query_turned = rotate(query_vectors, positions)
    key_turned = rotate(key_vectors, positions)
    head_chunks = jnp.stack([query_turned, key_turned, value_vectors]).reshape(
        3, tok_rows, member_count, model_width // member_count
    )
    qkv_group = lax.all_to_all(
        head_chunks.transpose(0, 2, 1, 3), MEMBER, split_axis=1, concat_axis=2, tiled=True
    )
    query_group, key_group, value_group = qkv_group[0, 0], qkv_group[1, 0], qkv_group[2, 0]
    column_count = key_group.shape[1]
    stacked = jnp.stack(
        [
            key_group.reshape(page_count, PAGE, column_count),
            value_group.reshape(page_count, PAGE, column_count),
        ],
        axis=1,
    ).reshape(page_count, -1)
    owner_of_page = my_pages // page_count
    group_range = jnp.arange(req_count, dtype=jnp.int32)
    page_range = jnp.arange(page_count, dtype=jnp.int32)
    page_blocks = stacked.reshape(page_count, 2, PAGE, column_count)
    sends_to = owner_of_page[None, :] == group_range[:, None]
    page_for_group = jnp.sum(jnp.where(sends_to, page_range[None, :], 0), axis=1)
    outgoing_pages = jnp.where(
        jnp.any(sends_to, axis=1)[:, None, None, None], page_blocks[page_for_group], jnp.zeros_like(page_blocks[:1])
    )
    incoming_pages = lax.all_to_all(outgoing_pages, "req", split_axis=0, concat_axis=0, tiled=True)
    source_holds = (request_groups[None, :] == group_range[:, None]).astype(jnp.int32)
    source_pages = jnp.sum(source_holds[:, :, None] * page_table[None, :, :], axis=1)
    slot_ids = group * page_count + page_range
    slot_source = jnp.sum(
        jnp.where(
            jnp.any(source_pages[None, :, :] == slot_ids[:, None, None], axis=2), group_range[None, :], 0
        ),
        axis=1,
    )
    kv_pages = incoming_pages[slot_source]
    heads_here = column_count // HEAD
    query_heads = query_group.reshape(group_rows, heads_here, HEAD)
    key_heads = key_group.reshape(group_rows, heads_here, HEAD)
    value_heads = value_group.reshape(group_rows, heads_here, HEAD)
    block_rows = group_rows
    attended = attend_all(query_heads, key_heads, value_heads, segment_ids, block_rows)
    token_heads = lax.all_to_all(attended, MEMBER, split_axis=0, concat_axis=1, tiled=True)
    hidden = residual.astype(jnp.float32) + jnp.dot(
        token_heads, out_weight, preferred_element_type=jnp.float32
    )
    normed = (
        hidden * lax.rsqrt(jnp.mean(hidden * hidden, axis=-1, keepdims=True) + norm_eps) * norm_gain
    ).astype(jnp.bfloat16)
    partner_inner, partner_outer, normed = lax.optimization_barrier((partner_inner, partner_outer, normed))
    expert_range = jnp.arange(expert_count, dtype=jnp.int32)
    chosen = (expert_ids[:, :, None] == expert_range[None, None, :]).astype(jnp.int32)
    picked = jnp.sum(chosen, axis=1)
    earlier = jnp.cumsum(picked, axis=0) - picked
    slot_rank = jnp.sum(chosen * earlier[:, None, :], axis=2)
    slot_index = expert_ids * capacity + slot_rank
    slot_range = jnp.arange(expert_count * capacity, dtype=jnp.int32)
    dispatch_matrix = jnp.sum(
        (slot_index[None, :, :] == slot_range[:, None, None]).astype(jnp.int32), axis=2
    ).astype(jnp.bfloat16)
    packed = (
        jnp.dot(dispatch_matrix, normed, preferred_element_type=jnp.float32)
        .astype(jnp.bfloat16)
        .reshape(expert_count, capacity, model_width)
    )
    expert_input = send_rows(packed)
    flat_input = expert_input.reshape(expert_count * capacity, model_width)
    inner_both = jnp.concatenate([expert_inner[0], partner_inner[0]], axis=1)
    outer_both = jnp.concatenate([expert_outer[0], partner_outer[0]], axis=0)
    expert_out = full_expert(flat_input, inner_both, outer_both).reshape(
        expert_count, capacity, model_width
    )
    returned = send_back(expert_out).reshape(expert_count * capacity, model_width)
    combine = jnp.sum(
        jnp.where(slot_index[:, :, None] == slot_range[None, None, :], gate_weights[:, :, None], 0.0),
        axis=1,
    )
    combine_high = combine.astype(jnp.bfloat16)
    combine_low = (combine - combine_high.astype(jnp.float32)).astype(jnp.bfloat16)
    both_parts = jnp.dot(
        jnp.concatenate([combine_high, combine_low], axis=0), returned, preferred_element_type=jnp.float32
    )
    mixed = both_parts[:tok_rows] + both_parts[tok_rows:]
    layer_out = (hidden + mixed).astype(jnp.bfloat16)
    return (layer_out, kv_pages)


def solution(mesh):
    req_count, member_count = mesh.devices.shape
    fine = Mesh(mesh.devices.reshape(req_count, member_count // 2, 2), EVERY)
    token_rows = P(EVERY, None)
    placed = (
        token_rows,
        token_rows,
        token_rows,
        token_rows,
        P("req"),
        P(),
        P(),
        P(),
        token_rows,
        token_rows,
        P(),
        P(),
        P(EVERY, None, None),
        P(EVERY, None, None),
    )
    return jax.shard_map(
        on_device,
        mesh=fine,
        in_specs=placed,
        out_specs=(token_rows, P("req", None, None, MEMBER)),
        check_vma=False,
    )
```

```python
import jax
import jax.numpy as jnp
from jax import lax
from jax.sharding import Mesh, PartitionSpec as P

HEAD = 128
PAGE = 128
MEMBER = ("x", "core")
EXPERT_AXES = ("req", "x")
EVERY = ("req", "x", "core")


rope_base = 10000.0
norm_eps = 1e-06
masked_score = -1e30


def partner(value, axis, distance):
    return lax.ppermute(value, axis, [(i, i ^ 1 << distance) for i in range(lax.axis_size(axis))])


def rotate(values_in, positions):
    row_count = values_in.shape[0]
    half_head = HEAD // 2
    inverse = rope_base ** (-(2.0 * jnp.arange(half_head, dtype=jnp.float32)) / HEAD)
    angles = positions[:, None] * inverse[None, :]
    cosine = jnp.cos(angles)[:, None, :]
    sines = jnp.sin(angles)[:, None, :]
    shaped = values_in.astype(jnp.float32).reshape(row_count, -1, HEAD)
    first_half = shaped[..., :half_head]
    second_half = shaped[..., half_head:]
    turned = jnp.concatenate(
        [first_half * cosine - second_half * sines, second_half * cosine + first_half * sines],
        axis=-1,
    )
    return turned.reshape(row_count, -1).astype(jnp.bfloat16)


def score_block(query_block, query_segments, key_block, key_segments):
    scores = jnp.einsum(
        "qhd,khd->hqk", query_block, key_block, preferred_element_type=jnp.float32
    ) * HEAD ** (-0.5)
    same_prompt = (query_segments[:, None] == key_segments[None, :])[None]
    return (jnp.where(same_prompt, scores, masked_score), same_prompt)


def attend_all(query_heads, key_heads, value_heads, group_segments, block_rows):
    block_count = query_heads.shape[0] // block_rows

    def one_block(block_index):
        start_row = block_index * block_rows
        query_block = lax.dynamic_slice_in_dim(query_heads, start_row, block_rows, 0)
        query_segments = lax.dynamic_slice_in_dim(group_segments, start_row, block_rows, 0)
        scores, same_prompt = score_block(query_block, query_segments, key_heads, group_segments)
        top_score = jnp.max(scores, axis=-1, keepdims=True)
        weights = jnp.where(same_prompt, jnp.exp(scores - top_score), 0.0)
        totals = jnp.sum(weights, axis=-1)
        mixed = jnp.einsum(
            "hqk,khd->qhd",
            weights.astype(jnp.bfloat16),
            value_heads,
            preferred_element_type=jnp.float32,
        )
        return (mixed / totals.T[:, :, None]).astype(jnp.bfloat16)

    results = lax.map(one_block, jnp.arange(block_count))
    return results.reshape(query_heads.shape[0], -1)


def send_rows(blocks):
    arrived = lax.all_to_all(blocks, EXPERT_AXES, split_axis=0, concat_axis=0, tiled=True)
    return arrived


def send_back(blocks):
    arrived = lax.all_to_all(blocks, EXPERT_AXES, split_axis=0, concat_axis=0, tiled=True)
    return arrived


def full_expert(rows, inner_both, outer_both):
    projected = jnp.dot(rows, inner_both, preferred_element_type=jnp.float32)
    quarter = projected.shape[1] // 4
    active = jnp.concatenate(
        [
            jax.nn.silu(projected[:, :quarter]) * projected[:, quarter : 2 * quarter],
            jax.nn.silu(projected[:, 2 * quarter : 3 * quarter]) * projected[:, 3 * quarter :],
        ],
        axis=1,
    ).astype(jnp.bfloat16)
    return jnp.dot(active, outer_both, preferred_element_type=jnp.float32).astype(jnp.bfloat16)


def on_device(
    residual,
    query_vectors,
    key_vectors,
    value_vectors,
    segment_ids,
    prompt_lengths,
    request_groups,
    page_table,
    expert_ids,
    gate_weights,
    out_weight,
    norm_gain,
    expert_inner,
    expert_outer,
):
    partner_inner = partner(expert_inner, "core", 0)
    partner_outer = partner(expert_outer, "core", 0)
    tok_rows, model_width = residual.shape
    req_count = lax.axis_size("req")
    member_count = lax.axis_size("x") * lax.axis_size("core")
    device_count = req_count * member_count
    expert_count = device_count // 2
    group_rows = tok_rows * member_count
    top_count = expert_ids.shape[1]
    capacity = 3 * tok_rows * top_count // (2 * expert_count)
    page_count = group_rows // PAGE
    group = lax.axis_index("req")
    member = lax.axis_index(MEMBER)
    holds_request = (request_groups == group).astype(jnp.int32)
    my_lengths = jnp.sum(holds_request[:, None] * prompt_lengths, axis=0)
    my_pages = jnp.sum(holds_request[:, None] * page_table, axis=0)
    starts = jnp.cumsum(my_lengths) - my_lengths
    first_row = member * tok_rows
    my_segments = lax.dynamic_slice_in_dim(segment_ids, first_row, tok_rows, 0)
    prompt_index = jnp.arange(prompt_lengths.shape[1], dtype=jnp.int32)
    token_start = jnp.sum(
        jnp.where(my_segments[:, None] == prompt_index[None, :], starts[None, :], 0), axis=1
    )
    positions = (first_row + jnp.arange(tok_rows, dtype=jnp.int32) - token_start).astype(
        jnp.float32
    )
    query_turned = rotate(query_vectors, positions)
    key_turned = rotate(key_vectors, positions)
    head_chunks = jnp.stack([query_turned, key_turned, value_vectors]).reshape(
        3, tok_rows, member_count, model_width // member_count
    )
    qkv_group = lax.all_to_all(
        head_chunks.transpose(0, 2, 1, 3), MEMBER, split_axis=1, concat_axis=2, tiled=True
    )
    query_group, key_group, value_group = qkv_group[0, 0], qkv_group[1, 0], qkv_group[2, 0]
    column_count = key_group.shape[1]
    stacked = jnp.stack(
        [
            key_group.reshape(page_count, PAGE, column_count),
            value_group.reshape(page_count, PAGE, column_count),
        ],
        axis=1,
    ).reshape(page_count, -1)
    owner_of_page = my_pages // page_count
    group_range = jnp.arange(req_count, dtype=jnp.int32)
    page_range = jnp.arange(page_count, dtype=jnp.int32)
    page_blocks = stacked.reshape(page_count, 2, PAGE, column_count)
    sends_to = owner_of_page[None, :] == group_range[:, None]
    page_for_group = jnp.sum(jnp.where(sends_to, page_range[None, :], 0), axis=1)
    outgoing_pages = jnp.where(
        jnp.any(sends_to, axis=1)[:, None, None, None], page_blocks[page_for_group], jnp.zeros_like(page_blocks[:1])
    )
    incoming_pages = lax.all_to_all(outgoing_pages, "req", split_axis=0, concat_axis=0, tiled=True)
    source_holds = (request_groups[None, :] == group_range[:, None]).astype(jnp.int32)
    source_pages = jnp.sum(source_holds[:, :, None] * page_table[None, :, :], axis=1)
    slot_ids = group * page_count + page_range
    slot_source = jnp.sum(
        jnp.where(
            jnp.any(source_pages[None, :, :] == slot_ids[:, None, None], axis=2), group_range[None, :], 0
        ),
        axis=1,
    )
    kv_pages = incoming_pages[slot_source]
    heads_here = column_count // HEAD
    query_heads = query_group.reshape(group_rows, heads_here, HEAD)
    key_heads = key_group.reshape(group_rows, heads_here, HEAD)
    value_heads = value_group.reshape(group_rows, heads_here, HEAD)
    block_rows = group_rows
    attended = attend_all(query_heads, key_heads, value_heads, segment_ids, block_rows)
    token_heads = lax.all_to_all(attended, MEMBER, split_axis=0, concat_axis=1, tiled=True)
    hidden = residual.astype(jnp.float32) + jnp.dot(
        token_heads, out_weight, preferred_element_type=jnp.float32
    )
    normed = (
        hidden * lax.rsqrt(jnp.mean(hidden * hidden, axis=-1, keepdims=True) + norm_eps) * norm_gain
    ).astype(jnp.bfloat16)
    partner_inner, partner_outer, normed = lax.optimization_barrier((partner_inner, partner_outer, normed))
    expert_range = jnp.arange(expert_count, dtype=jnp.int32)
    chosen = (expert_ids[:, :, None] == expert_range[None, None, :]).astype(jnp.int32)
    picked = jnp.sum(chosen, axis=1)
    earlier = jnp.cumsum(picked, axis=0) - picked
    slot_rank = jnp.sum(chosen * earlier[:, None, :], axis=2)
    slot_index = expert_ids * capacity + slot_rank
    slot_range = jnp.arange(expert_count * capacity, dtype=jnp.int32)
    dispatch_matrix = jnp.sum(
        (slot_index[None, :, :] == slot_range[:, None, None]).astype(jnp.int32), axis=2
    ).astype(jnp.bfloat16)
    packed = (
        jnp.dot(dispatch_matrix, normed, preferred_element_type=jnp.float32)
        .astype(jnp.bfloat16)
        .reshape(expert_count, capacity, model_width)
    )
    expert_input = send_rows(packed)
    flat_input = expert_input.reshape(expert_count * capacity, model_width)
    inner_both = jnp.concatenate([expert_inner[0], partner_inner[0]], axis=1)
    outer_both = jnp.concatenate([expert_outer[0], partner_outer[0]], axis=0)
    expert_out = full_expert(flat_input, inner_both, outer_both).reshape(
        expert_count, capacity, model_width
    )
    returned = send_back(expert_out).reshape(expert_count * capacity, model_width)
    combine = jnp.sum(
        jnp.where(slot_index[:, :, None] == slot_range[None, None, :], gate_weights[:, :, None], 0.0),
        axis=1,
    )
    mixed = jnp.dot(combine.astype(jnp.bfloat16), returned, preferred_element_type=jnp.float32)
    layer_out = (hidden + mixed).astype(jnp.bfloat16)
    return (layer_out, kv_pages)


def solution(mesh):
    req_count, member_count = mesh.devices.shape
    fine = Mesh(mesh.devices.reshape(req_count, member_count // 2, 2), EVERY)
    token_rows = P(EVERY, None)
    placed = (
        token_rows,
        token_rows,
        token_rows,
        token_rows,
        P("req"),
        P(),
        P(),
        P(),
        token_rows,
        token_rows,
        P(),
        P(),
        P(EVERY, None, None),
        P(EVERY, None, None),
    )
    return jax.shard_map(
        on_device,
        mesh=fine,
        in_specs=placed,
        out_specs=(token_rows, P("req", None, None, MEMBER)),
        check_vma=False,
    )
```
